32 devices in a mesh: row: 4 (over y, x), col: 8 (over z, core).
Axes of the slice: x: 2, y: 2, z: 4, core: 2. Of those that a mesh axis runs over, the one named last changes fastest.
Arguments:
- tiles: bfloat16 [64, 128, 128, 128], P('row', 'col'), may hold values from -1 to 1
- tile_cols: int32 [64, 128], P('row', 'col'), may hold values from 0 to 7
- degree_scale: float32 [8192], P(('row', 'col')), may hold values from 0.8 to 1.25
- start_block: float32 [8192, 128], P(('row', 'col')), may hold values from -9 to 9
- planted: bfloat16 [8192, 128], P(('row', 'col')), may hold values from -19.595918 to 19.595918
- strengths: float32 [128], replicated, may hold values from 1.5 to 2.1
- bounds: float32 [2], replicated, may hold values from -2.2 to 1.7, as said below
Outputs:
- ortho_basis: float32 [8192, 128], P(('row', 'col'))
- projected: float32 [128, 128], replicated
The draws below stay inside these ranges and needn't reach their ends.
Inputs may be any that keep to these rules, and one draw needn't show every extreme that they name: bounds[0] is the lower end and bounds[1] the upper end; bounds[1] - bounds[0] is at least 3.
All inputs are finite; a program needn't handle non-finite values.
Results may differ from the reference program's by a relative error of at most 0.038.
Values may be sent and summed in bfloat16 or wider, within the bound.
No kernel may reach another device: no remote copies, remote signals or barrier semaphores. Data moves between devices by JAX's collectives and lax.ppermute only.
A program may use at most 128 MiB of HBM per device.

```python
import math
import jax
import jax.numpy as jnp
from jax import lax

TILE = 128
BLOCK = 128
PIECE = 256
SLOTS = 16
DEGREE = 4
NODES = 8192
TILE_ROWS = 64
COL_TILES = 8
N_COL = 8


def draw_tiles(key, part):
    spread = (3.0 * N_COL * SLOTS * TILE) ** (-0.5)
    shape = (TILE_ROWS, N_COL * SLOTS, TILE, TILE)
    values = jnp.clip(jax.random.normal(key, shape, jnp.float32), -4.0, 4.0)
    return (values * spread).astype(jnp.bfloat16)


def draw_start_block(key, part):
    value_key = jax.random.fold_in(key, 0)
    values = jnp.clip(jax.random.normal(value_key, (NODES, BLOCK), jnp.float32), -5.0, 5.0)
    return (values + 0.8 * jnp.roll(values, 1, axis=1)).astype(jnp.float32)


def draw_planted(key, part):
    value_key, shift_key = jax.random.split(jax.random.fold_in(key, 7))
    groups = NODES // PIECE
    offset = jax.random.randint(shift_key, (), 0, groups)
    home = (jnp.arange(NODES, dtype=jnp.int32) // PIECE + offset) % groups
    column = jnp.arange(BLOCK, dtype=jnp.int32) % groups
    heavy = home[:, None] == column[None, :]
    values = jnp.clip(jax.random.normal(value_key, (NODES, BLOCK), jnp.float32), -4.0, 4.0)
    boost = (0.75 * NODES / PIECE) ** 0.5
    scale = jnp.where(heavy, jnp.float32(boost), jnp.float32(0.5))
    return (values * scale).astype(jnp.bfloat16)


def draw_bounds(key, part):
    low_key, high_key = jax.random.split(key)
    lower_end = jax.random.uniform(low_key, (), jnp.float32, -2.2, -1.8)
    upper_end = jax.random.uniform(high_key, (), jnp.float32, 1.3, 1.7)
    return jnp.stack([lower_end, upper_end]).astype(jnp.float32)


def place_ends(array, rng, low, high):
    longest = array.shape.index(max(array.shape))
    spots = []
    for shift in (0, 1):
        where = [jax.random.randint(jax.random.fold_in(rng, axis), (), 0, length) for axis, length in enumerate(array.shape)]
        where[longest] = (where[longest] + shift) % array.shape[longest]
        spots.append(tuple(where))
    return array.at[spots[0]].set(low).at[spots[1]].set(high)


def steps_of(stream_key, dims, pieces, low, top_value):
    loudness, own = 1.0, jax.random.fold_in(stream_key, 6)
    for dim, shards_of in pieces:
        heights = jnp.exp(jax.random.uniform(jax.random.fold_in(own, dim), (shards_of,), jnp.float32, low / len(pieces), top_value / len(pieces)))
        loudness = loudness * jnp.repeat(heights, dims[dim] // shards_of).reshape([-1 if axis == dim else 1 for axis in range(len(dims))])
    return loudness


def setup_inputs(seed: int = 0) -> dict:
    key_list = jax.random.split(jax.random.key(seed), 8)
    return {
        "tiles": draw_tiles(jax.random.fold_in(key_list[7], 71), 0),
        "tile_cols": place_ends(jax.random.randint(key_list[1], (TILE_ROWS, N_COL * SLOTS), 0, COL_TILES), jax.random.fold_in(key_list[1], 1), 0, COL_TILES - 1).astype(jnp.int32),
        "degree_scale": jnp.clip(jnp.exp(math.log(1.25) - 0.4462871 * jax.random.uniform(key_list[2], (NODES,), jnp.float32) ** steps_of(key_list[2], (NODES,), ((0, 32),), -0.2, 0.2)), 0.8, 1.25),
        "start_block": draw_start_block(jax.random.fold_in(key_list[7], 71), 0),
        "planted": draw_planted(jax.random.fold_in(key_list[7], 71), 0),
        "strengths": jnp.clip(jax.random.uniform(key_list[5], (BLOCK,), jnp.float32, 1.5, 2.1), 1.5, 2.1),
        "bounds": draw_bounds(jax.random.fold_in(key_list[7], 71), 0),
    }


def operate(vector, tiles, tile_cols, degree_scale, planted, strengths):
    scaled = (degree_scale[:, None] * vector).astype(jnp.bfloat16)
    coupling = jnp.dot(planted.T.astype(jnp.float32), scaled.astype(jnp.float32), preferred_element_type=jnp.float32)
    per_piece = PIECE // TILE
    owner_dev = (jnp.arange(N_COL * SLOTS, dtype=jnp.int32) // SLOTS).astype(jnp.int32)
    global_cols = ((tile_cols // per_piece * N_COL + owner_dev[None, :]) * per_piece + tile_cols % per_piece).astype(jnp.int32)
    blocks = scaled.reshape(TILE_ROWS, TILE, BLOCK)

    def one_row(pair):
        row_tiles, row_cols = pair
        picked = blocks[row_cols].astype(jnp.float32)
        return jnp.einsum('sab,sbk->ak', row_tiles.astype(jnp.float32), picked)
    product = lax.map(one_row, (tiles, global_cols)).reshape(NODES, BLOCK)
    lifted = jnp.dot(planted.astype(jnp.float32), strengths[:, None] * coupling, precision=lax.Precision.HIGHEST) / NODES
    return degree_scale[:, None] * (product + lifted)

def reference(tiles, tile_cols, degree_scale, start_block, planted, strengths, bounds):
    center = (bounds[1] + bounds[0]) * 0.5
    half_width = (bounds[1] - bounds[0]) * 0.5
    previous = start_block
    current = (operate(start_block, tiles, tile_cols, degree_scale, planted, strengths) - center * start_block) / half_width
    for index_step in range(DEGREE - 1):
        applied = operate(current, tiles, tile_cols, degree_scale, planted, strengths)
        following = 2.0 * (applied - center * current) / half_width - previous
        previous, current = (current, following)
    gram_matrix = jnp.dot(current.T, current, precision=lax.Precision.HIGHEST) / NODES
    factor = jnp.linalg.cholesky(gram_matrix)
    ortho_basis = lax.linalg.triangular_solve(factor, current, left_side=False, lower=True, transpose_a=True)
    applied = operate(current, tiles, tile_cols, degree_scale, planted, strengths)
    rayleigh = jnp.dot(current.T, applied, precision=lax.Precision.HIGHEST) / NODES
    half_solved = lax.linalg.triangular_solve(factor, rayleigh, left_side=True, lower=True)
    projected = lax.linalg.triangular_solve(factor, half_solved, left_side=False, lower=True, transpose_a=True)
    return (ortho_basis, projected)
```

```python
import jax
import jax.numpy as jnp
from jax import lax
from jax.sharding import PartitionSpec as P

DEGREE = 4


def split_bf16(value):
    upper = value.astype(jnp.bfloat16)
    lower = (value - upper.astype(jnp.float32)).astype(jnp.bfloat16)
    return upper, lower


def split_dot(left, right_f32):
    upper, lower = split_bf16(right_f32)
    first = jnp.dot(left, upper, preferred_element_type=jnp.float32)
    return first + jnp.dot(left, lower, preferred_element_type=jnp.float32)


def local(tiles, tile_cols, degree_scale, start_block, planted, strengths, bounds):
    piece_rows = start_block.shape[0]
    node_count = piece_rows * lax.axis_size("row") * lax.axis_size("col")
    tile_rows, slots, tile_size = tiles.shape[0], tiles.shape[1], tiles.shape[2]
    n_blocks = lax.axis_size("row") * piece_rows // tile_size
    weights = strengths[:, None]

    onehot = (tile_cols[:, :, None] == jnp.arange(n_blocks, dtype=jnp.int32)[None, None, :]).astype(jnp.bfloat16)
    dense = jnp.einsum("rst,rsab->ratb", onehot, tiles, preferred_element_type=jnp.float32)
    dense = dense.reshape(tile_rows * tile_size, n_blocks * tile_size)
    w_hi, w_lo = split_bf16(dense)

    planted_cols = lax.all_gather(planted, "row", axis=0, tiled=True)
    planted_rows = lax.all_gather(planted, "col", axis=0, tiled=True)

    def operate(vector):
        scaled = (degree_scale[:, None] * vector).astype(jnp.bfloat16)
        gathered = lax.all_gather(scaled, "row", axis=0, tiled=True)
        product = jnp.dot(w_hi, gathered, preferred_element_type=jnp.float32)
        product = product + jnp.dot(w_lo, gathered, preferred_element_type=jnp.float32)
        partial = lax.dot_general(
            planted_cols, gathered, (((0,), (0,)), ((), ())), preferred_element_type=jnp.float32
        )
        product = product + split_dot(planted_rows, weights * partial) / node_count
        summed = lax.psum_scatter(product, "col", scatter_dimension=0, tiled=True)
        return degree_scale[:, None] * summed

    center = (bounds[1] + bounds[0]) * 0.5
    half_width = (bounds[1] - bounds[0]) * 0.5
    previous = start_block
    current = (operate(start_block) - center * start_block) / half_width
    for index_step in range(DEGREE - 1):
        applied = operate(current)
        following = 2.0 * (applied - center * current) / half_width - previous
        previous, current = (current, following)
    local_gram = jnp.dot(current.T, current, precision=lax.Precision.HIGHEST)
    applied = operate(current)
    local_rayleigh = jnp.dot(current.T, applied, precision=lax.Precision.HIGHEST)
    gram_total, rayleigh_total = lax.psum((local_gram, local_rayleigh), ("row", "col"))
    gram_matrix = gram_total / node_count
    rayleigh = rayleigh_total / node_count
    factor = jnp.linalg.cholesky(gram_matrix)
    ortho_basis = lax.linalg.triangular_solve(
        factor, current, left_side=False, lower=True, transpose_a=True
    )
    half_solved = lax.linalg.triangular_solve(factor, rayleigh, left_side=True, lower=True)
    projected = lax.linalg.triangular_solve(
        factor, half_solved, left_side=False, lower=True, transpose_a=True
    )
    return (ortho_basis, projected)


def solution(mesh):
    in_specs = (
        P("row", "col", None, None),
        P("row", "col"),
        P(("row", "col")),
        P(("row", "col"), None),
        P(("row", "col"), None),
        P(),
        P(),
    )
    out_specs = (P(("row", "col"), None), P())
    return jax.shard_map(local, mesh=mesh, in_specs=in_specs, out_specs=out_specs, check_vma=False)
```

```python
import jax
import jax.numpy as jnp
from jax import lax
from jax.sharding import PartitionSpec as P

DEGREE = 4


def split_bf16(value):
    upper = value.astype(jnp.bfloat16)
    lower = (value - upper.astype(jnp.float32)).astype(jnp.bfloat16)
    return upper, lower


def split_dot(left, right_f32):
    upper, lower = split_bf16(right_f32)
    first = jnp.dot(left, upper, preferred_element_type=jnp.float32)
    return first + jnp.dot(left, lower, preferred_element_type=jnp.float32)


def butterfly_sum(value, axis):
    size = lax.axis_size(axis)
    if size & (size - 1):
        return lax.psum(value, axis)
    step = 1
    while step < size:
        pairs = [(index, index ^ step) for index in range(size)]
        value = value + lax.ppermute(value, axis, pairs)
        step *= 2
    return value


def all_sum(value):
    return butterfly_sum(butterfly_sum(value, "col"), "row")


def scatter_sum(value, axis):
    size = lax.axis_size(axis)
    here = lax.axis_index(axis)
    blocks = value.reshape(size, value.shape[0] // size, value.shape[1])
    total = jnp.take(blocks, here, axis=0)
    for shift in range(1, size):
        part = jnp.take(blocks, (here + shift) % size, axis=0)
        pairs = [(index, (index + shift) % size) for index in range(size)]
        total = total + lax.ppermute(part, axis, pairs)
    return total


def local(tiles, tile_cols, degree_scale, start_block, planted, strengths, bounds):
    piece_rows = start_block.shape[0]
    node_count = piece_rows * lax.axis_size("row") * lax.axis_size("col")
    tile_rows, slots, tile_size = tiles.shape[0], tiles.shape[1], tiles.shape[2]
    n_blocks = lax.axis_size("row") * piece_rows // tile_size
    weights = strengths[:, None]

    onehot = (tile_cols[:, :, None] == jnp.arange(n_blocks, dtype=jnp.int32)[None, None, :]).astype(jnp.bfloat16)
    dense = jnp.einsum("rst,rsab->ratb", onehot, tiles, preferred_element_type=jnp.float32)
    dense = dense.reshape(tile_rows * tile_size, n_blocks * tile_size)
    w_hi, w_lo = split_bf16(dense)

    planted_cols = lax.all_gather(planted, "row", axis=0, tiled=True)
    planted_rows = lax.all_gather(planted, "col", axis=0, tiled=True)

    def operate(vector):
        scaled = (degree_scale[:, None] * vector).astype(jnp.bfloat16)
        gathered = lax.all_gather(scaled, "row", axis=0, tiled=True)
        product = jnp.dot(w_hi, gathered, preferred_element_type=jnp.float32)
        product = product + jnp.dot(w_lo, gathered, preferred_element_type=jnp.float32)
        partial = lax.dot_general(
            planted_cols, gathered, (((0,), (0,)), ((), ())), preferred_element_type=jnp.float32
        )
        product = product + split_dot(planted_rows, weights * partial) / node_count
        summed = scatter_sum(product, "col")
        return degree_scale[:, None] * summed

    center = (bounds[1] + bounds[0]) * 0.5
    half_width = (bounds[1] - bounds[0]) * 0.5
    previous = start_block
    current = (operate(start_block) - center * start_block) / half_width
    for index_step in range(DEGREE - 1):
        applied = operate(current)
        following = 2.0 * (applied - center * current) / half_width - previous
        previous, current = (current, following)
    local_gram = jnp.dot(current.T, current, precision=lax.Precision.HIGHEST)
    gram_total = all_sum(local_gram)
    applied = operate(current)
    local_rayleigh = jnp.dot(current.T, applied, precision=lax.Precision.HIGHEST)
    rayleigh_total = all_sum(local_rayleigh)
    gram_matrix = gram_total / node_count
    rayleigh = rayleigh_total / node_count
    factor = jnp.linalg.cholesky(gram_matrix)
    ortho_basis = lax.linalg.triangular_solve(
        factor, current, left_side=False, lower=True, transpose_a=True
    )
    half_solved = lax.linalg.triangular_solve(factor, rayleigh, left_side=True, lower=True)
    projected = lax.linalg.triangular_solve(
        factor, half_solved, left_side=False, lower=True, transpose_a=True
    )
    return (ortho_basis, projected)


def solution(mesh):
    in_specs = (
        P("row", "col", None, None),
        P("row", "col"),
        P(("row", "col")),
        P(("row", "col"), None),
        P(("row", "col"), None),
        P(),
        P(),
    )
    out_specs = (P(("row", "col"), None), P())
    return jax.shard_map(local, mesh=mesh, in_specs=in_specs, out_specs=out_specs, check_vma=False)
```

```python
import jax
import jax.numpy as jnp
from jax import lax
from jax.sharding import PartitionSpec as P

DEGREE = 4


def split_bf16(value):
    upper = value.astype(jnp.bfloat16)
    lower = (value - upper.astype(jnp.float32)).astype(jnp.bfloat16)
    return upper, lower


def split_dot(left, right_f32):
    upper, lower = split_bf16(right_f32)
    first = jnp.dot(left, upper, preferred_element_type=jnp.float32)
    return first + jnp.dot(left, lower, preferred_element_type=jnp.float32)


def butterfly_sum(value, axis):
    size = lax.axis_size(axis)
    if size & (size - 1):
        return lax.psum(value, axis)
    step = 1
    while step < size:
        pairs = [(index, index ^ step) for index in range(size)]
        value = value + lax.ppermute(value, axis, pairs)
        step *= 2
    return value


def all_sum(value):
    return butterfly_sum(butterfly_sum(value, "col"), "row")


def scatter_sum(value, axis):
    size = lax.axis_size(axis)
    here = lax.axis_index(axis)
    blocks = value.reshape(size, value.shape[0] // size, value.shape[1])
    total = jnp.take(blocks, here, axis=0)
    for shift in range(1, size):
        part = jnp.take(blocks, (here + shift) % size, axis=0)
        pairs = [(index, (index + shift) % size) for index in range(size)]
        total = total + lax.ppermute(part, axis, pairs)
    return total


def halving_scatter_sum(value, axis):
    size = lax.axis_size(axis)
    if size & (size - 1):
        return scatter_sum(value, axis)
    here = lax.axis_index(axis)
    rows = value.shape[0] // size
    blocks = value.reshape(size, rows, value.shape[1])
    step = 1
    while step < size:
        bit = (here // step) % 2
        paired = blocks.reshape(blocks.shape[0] // 2, 2, rows, value.shape[1])
        kept = lax.dynamic_index_in_dim(paired, bit, axis=1, keepdims=False)
        sent = lax.dynamic_index_in_dim(paired, 1 - bit, axis=1, keepdims=False)
        pairs = [(index, index ^ step) for index in range(size)]
        blocks = kept + lax.ppermute(sent, axis, pairs)
        step *= 2
    return blocks.reshape(rows, value.shape[1])


def doubling_gather(value, axis):
    size = lax.axis_size(axis)
    if size & (size - 1):
        return lax.all_gather(value, axis, axis=0, tiled=True)
    here = lax.axis_index(axis)
    result = value
    step = 1
    while step < size:
        pairs = [(index, index ^ step) for index in range(size)]
        other = lax.ppermute(result, axis, pairs)
        low = (here // step) % 2 == 0
        result = jnp.concatenate(
            [jnp.where(low, result, other), jnp.where(low, other, result)], axis=0
        )
        step *= 2
    return result


def local(tiles, tile_cols, degree_scale, start_block, planted, strengths, bounds):
    piece_rows = start_block.shape[0]
    node_count = piece_rows * lax.axis_size("row") * lax.axis_size("col")
    tile_rows, slots, tile_size = tiles.shape[0], tiles.shape[1], tiles.shape[2]
    n_blocks = lax.axis_size("row") * piece_rows // tile_size
    weights = strengths[:, None]

    onehot = (tile_cols[:, :, None] == jnp.arange(n_blocks, dtype=jnp.int32)[None, None, :]).astype(jnp.bfloat16)
    dense = jnp.einsum("rst,rsab->ratb", onehot, tiles, preferred_element_type=jnp.float32)
    dense = dense.reshape(tile_rows * tile_size, n_blocks * tile_size)
    w_hi, w_lo = split_bf16(dense)

    planted_cols = doubling_gather(planted, "row")
    planted_rows = doubling_gather(planted, "col")

    def operate(vector):
        scaled = (degree_scale[:, None] * vector).astype(jnp.bfloat16)
        gathered = doubling_gather(scaled, "row")
        product = jnp.dot(w_hi, gathered, preferred_element_type=jnp.float32)
        product = product + jnp.dot(w_lo, gathered, preferred_element_type=jnp.float32)
        partial = lax.dot_general(
            planted_cols, gathered, (((0,), (0,)), ((), ())), preferred_element_type=jnp.float32
        )
        product = product + split_dot(planted_rows, weights * partial) / node_count
        summed = halving_scatter_sum(product, "col")
        return degree_scale[:, None] * summed

    center = (bounds[1] + bounds[0]) * 0.5
    half_width = (bounds[1] - bounds[0]) * 0.5
    previous = start_block
    current = (operate(start_block) - center * start_block) / half_width
    for index_step in range(DEGREE - 1):
        applied = operate(current)
        following = 2.0 * (applied - center * current) / half_width - previous
        previous, current = (current, following)
    local_gram = jnp.dot(current.T, current, precision=lax.Precision.HIGHEST)
    gram_total = all_sum(local_gram)
    applied = operate(current)
    local_rayleigh = jnp.dot(current.T, applied, precision=lax.Precision.HIGHEST)
    rayleigh_total = all_sum(local_rayleigh)
    gram_matrix = gram_total / node_count
    rayleigh = rayleigh_total / node_count
    factor = jnp.linalg.cholesky(gram_matrix)
    ortho_basis = lax.linalg.triangular_solve(
        factor, current, left_side=False, lower=True, transpose_a=True
    )
    half_solved = lax.linalg.triangular_solve(factor, rayleigh, left_side=True, lower=True)
    projected = lax.linalg.triangular_solve(
        factor, half_solved, left_side=False, lower=True, transpose_a=True
    )
    return (ortho_basis, projected)


def solution(mesh):
    in_specs = (
        P("row", "col", None, None),
        P("row", "col"),
        P(("row", "col")),
        P(("row", "col"), None),
        P(("row", "col"), None),
        P(),
        P(),
    )
    out_specs = (P(("row", "col"), None), P())
    return jax.shard_map(local, mesh=mesh, in_specs=in_specs, out_specs=out_specs, check_vma=False)
```

```python
import jax
import jax.numpy as jnp
from jax import lax
from jax.sharding import PartitionSpec as P

DEGREE = 4


def split_bf16(value):
    upper = value.astype(jnp.bfloat16)
    lower = (value - upper.astype(jnp.float32)).astype(jnp.bfloat16)
    return upper, lower


def split_dot(left, right_f32):
    upper, lower = split_bf16(right_f32)
    first = jnp.dot(left, upper, preferred_element_type=jnp.float32)
    return first + jnp.dot(left, lower, preferred_element_type=jnp.float32)


def butterfly_sum(value, axis):
    size = lax.axis_size(axis)
    if size & (size - 1):
        return lax.psum(value, axis)
    step = 1
    while step < size:
        pairs = [(index, index ^ step) for index in range(size)]
        value = value + lax.ppermute(value, axis, pairs)
        step *= 2
    return value


def all_sum(value):
    return butterfly_sum(butterfly_sum(value, "col"), "row")


def scatter_sum(value, axis):
    size = lax.axis_size(axis)
    here = lax.axis_index(axis)
    blocks = value.reshape(size, value.shape[0] // size, value.shape[1])
    total = jnp.take(blocks, here, axis=0)
    for shift in range(1, size):
        part = jnp.take(blocks, (here + shift) % size, axis=0)
        pairs = [(index, (index + shift) % size) for index in range(size)]
        total = total + lax.ppermute(part, axis, pairs)
    return total


def halving_scatter_sum(value, shared, axis):
    size = lax.axis_size(axis)
    if size & (size - 1):
        return scatter_sum(value, axis), lax.psum(shared, axis)
    here = lax.axis_index(axis)
    rows, width = value.shape[0] // size, value.shape[1]
    blocks = value.reshape(size, rows, width)
    step = 1
    while step < size:
        bit = (here // step) % 2
        paired = blocks.reshape(blocks.shape[0] // 2, 2, rows, width)
        kept = lax.dynamic_index_in_dim(paired, bit, axis=1, keepdims=False)
        sent = lax.dynamic_index_in_dim(paired, 1 - bit, axis=1, keepdims=False)
        payload = jnp.concatenate([sent.reshape(-1, width), shared], axis=0)
        pairs = [(index, index ^ step) for index in range(size)]
        got = lax.ppermute(payload, axis, pairs)
        blocks = kept + got[: kept.shape[0] * rows].reshape(kept.shape)
        shared = shared + got[kept.shape[0] * rows :]
        step *= 2
    return blocks.reshape(rows, width), shared


def doubling_gather(value, axis):
    size = lax.axis_size(axis)
    if size & (size - 1):
        return lax.all_gather(value, axis, axis=0, tiled=True)
    here = lax.axis_index(axis)
    result = value
    step = 1
    while step < size:
        pairs = [(index, index ^ step) for index in range(size)]
        other = lax.ppermute(result, axis, pairs)
        low = (here // step) % 2 == 0
        result = jnp.concatenate(
            [jnp.where(low, result, other), jnp.where(low, other, result)], axis=0
        )
        step *= 2
    return result


def local(tiles, tile_cols, degree_scale, start_block, planted, strengths, bounds):
    piece_rows = start_block.shape[0]
    node_count = piece_rows * lax.axis_size("row") * lax.axis_size("col")
    tile_rows, slots, tile_size = tiles.shape[0], tiles.shape[1], tiles.shape[2]
    n_blocks = lax.axis_size("row") * piece_rows // tile_size
    weights = strengths[:, None]

    onehot = (tile_cols[:, :, None] == jnp.arange(n_blocks, dtype=jnp.int32)[None, None, :]).astype(jnp.bfloat16)
    dense = jnp.einsum("rst,rsab->ratb", onehot, tiles, preferred_element_type=jnp.float32)
    dense = dense.reshape(tile_rows * tile_size, n_blocks * tile_size)
    w_hi, w_lo = split_bf16(dense)

    planted_cols = doubling_gather(planted, "row")

    def operate(vector):
        scaled = (degree_scale[:, None] * vector).astype(jnp.bfloat16)
        gathered = doubling_gather(scaled, "row")
        product = jnp.dot(w_hi, gathered, preferred_element_type=jnp.float32)
        product = product + jnp.dot(w_lo, gathered, preferred_element_type=jnp.float32)
        partial = lax.dot_general(
            planted_cols, gathered, (((0,), (0,)), ((), ())), preferred_element_type=jnp.float32
        )
        summed, lift = halving_scatter_sum(product, weights * partial / node_count, "col")
        summed = summed + split_dot(planted, lift)
        return degree_scale[:, None] * summed

    center = (bounds[1] + bounds[0]) * 0.5
    half_width = (bounds[1] - bounds[0]) * 0.5
    previous = start_block
    current = (operate(start_block) - center * start_block) / half_width
    for index_step in range(DEGREE - 1):
        applied = operate(current)
        following = 2.0 * (applied - center * current) / half_width - previous
        previous, current = (current, following)
    local_gram = jnp.dot(current.T, current, precision=lax.Precision.HIGHEST)
    gram_total = all_sum(local_gram)
    applied = operate(current)
    local_rayleigh = jnp.dot(current.T, applied, precision=lax.Precision.HIGHEST)
    rayleigh_total = all_sum(local_rayleigh)
    gram_matrix = gram_total / node_count
    rayleigh = rayleigh_total / node_count
    factor = jnp.linalg.cholesky(gram_matrix)
    ortho_basis = lax.linalg.triangular_solve(
        factor, current, left_side=False, lower=True, transpose_a=True
    )
    half_solved = lax.linalg.triangular_solve(factor, rayleigh, left_side=True, lower=True)
    projected = lax.linalg.triangular_solve(
        factor, half_solved, left_side=False, lower=True, transpose_a=True
    )
    return (ortho_basis, projected)


def solution(mesh):
    in_specs = (
        P("row", "col", None, None),
        P("row", "col"),
        P(("row", "col")),
        P(("row", "col"), None),
        P(("row", "col"), None),
        P(),
        P(),
    )
    out_specs = (P(("row", "col"), None), P())
    return jax.shard_map(local, mesh=mesh, in_specs=in_specs, out_specs=out_specs, check_vma=False)
```

```python
import jax
import jax.numpy as jnp
from jax import lax
from jax.sharding import PartitionSpec as P

DEGREE = 4


def split_bf16(value):
    upper = value.astype(jnp.bfloat16)
    lower = (value - upper.astype(jnp.float32)).astype(jnp.bfloat16)
    return upper, lower


def split_dot(left, right_f32):
    upper, lower = split_bf16(right_f32)
    first = jnp.dot(left, upper, preferred_element_type=jnp.float32)
    return first + jnp.dot(left, lower, preferred_element_type=jnp.float32)


def butterfly_sum(value, axis):
    size = lax.axis_size(axis)
    if size & (size - 1):
        return lax.psum(value, axis)
    step = 1
    while step < size:
        pairs = [(index, index ^ step) for index in range(size)]
        value = value + lax.ppermute(value, axis, pairs)
        step *= 2
    return value


def all_sum(value):
    return butterfly_sum(butterfly_sum(value, "col"), "row")


def scatter_sum(value, axis):
    size = lax.axis_size(axis)
    here = lax.axis_index(axis)
    blocks = value.reshape(size, value.shape[0] // size, value.shape[1])
    total = jnp.take(blocks, here, axis=0)
    for shift in range(1, size):
        part = jnp.take(blocks, (here + shift) % size, axis=0)
        pairs = [(index, (index + shift) % size) for index in range(size)]
        total = total + lax.ppermute(part, axis, pairs)
    return total


def halving_scatter_sum(value, axis):
    size = lax.axis_size(axis)
    if size & (size - 1):
        return scatter_sum(value, axis)
    here = lax.axis_index(axis)
    rows = value.shape[0] // size
    blocks = value.reshape(size, rows, value.shape[1])
    step = 1
    while step < size:
        bit = (here // step) % 2
        paired = blocks.reshape(blocks.shape[0] // 2, 2, rows, value.shape[1])
        kept = lax.dynamic_index_in_dim(paired, bit, axis=1, keepdims=False)
        sent = lax.dynamic_index_in_dim(paired, 1 - bit, axis=1, keepdims=False)
        pairs = [(index, index ^ step) for index in range(size)]
        blocks = kept + lax.ppermute(sent, axis, pairs)
        step *= 2
    return blocks.reshape(rows, value.shape[1])


def doubling_gather(value, axis):
    size = lax.axis_size(axis)
    if size & (size - 1):
        return lax.all_gather(value, axis, axis=0, tiled=True)
    here = lax.axis_index(axis)
    result = value
    step = 1
    while step < size:
        pairs = [(index, index ^ step) for index in range(size)]
        other = lax.ppermute(result, axis, pairs)
        low = (here // step) % 2 == 0
        result = jnp.concatenate(
            [jnp.where(low, result, other), jnp.where(low, other, result)], axis=0
        )
        step *= 2
    return result


def local(tiles, tile_cols, degree_scale, start_block, planted, strengths, bounds):
    piece_rows = start_block.shape[0]
    node_count = piece_rows * lax.axis_size("row") * lax.axis_size("col")
    tile_rows, slots, tile_size = tiles.shape[0], tiles.shape[1], tiles.shape[2]
    n_blocks = lax.axis_size("row") * piece_rows // tile_size
    weights = strengths[:, None]

    onehot = (tile_cols[:, :, None] == jnp.arange(n_blocks, dtype=jnp.int32)[None, None, :]).astype(jnp.bfloat16)
    dense = jnp.einsum("rst,rsab->ratb", onehot, tiles, preferred_element_type=jnp.float32)
    dense = dense.reshape(tile_rows * tile_size, n_blocks * tile_size)
    w_hi, w_lo = split_bf16(dense)

    planted_cols = doubling_gather(planted, "row")
    planted_rows = doubling_gather(planted, "col")

    def operate(vector):
        scaled = (degree_scale[:, None] * vector).astype(jnp.bfloat16)
        gathered = doubling_gather(scaled, "row")
        product = jnp.dot(w_hi, gathered, preferred_element_type=jnp.float32)
        product = product + jnp.dot(w_lo, gathered, preferred_element_type=jnp.float32)
        partial = lax.dot_general(
            planted_cols, gathered, (((0,), (0,)), ((), ())), preferred_element_type=jnp.float32
        )
        product = product + split_dot(planted_rows, weights * partial) / node_count
        summed = halving_scatter_sum(product, "col")
        return degree_scale[:, None] * summed

    center = (bounds[1] + bounds[0]) * 0.5
    half_width = (bounds[1] - bounds[0]) * 0.5
    previous = start_block
    current = (operate(start_block) - center * start_block) / half_width
    for index_step in range(DEGREE - 1):
        applied = operate(current)
        following = 2.0 * (applied - center * current) / half_width - previous
        previous, current = (current, following)
    local_gram = jnp.dot(current.T, current, precision=lax.Precision.HIGHEST)
    applied = operate(current)
    local_rayleigh = jnp.dot(current.T, applied, precision=lax.Precision.HIGHEST)
    totals = all_sum(jnp.concatenate([local_gram, local_rayleigh], axis=0))
    gram_total, rayleigh_total = totals[: local_gram.shape[0]], totals[local_gram.shape[0] :]
    gram_matrix = gram_total / node_count
    rayleigh = rayleigh_total / node_count
    factor = jnp.linalg.cholesky(gram_matrix)
    ortho_basis = lax.linalg.triangular_solve(
        factor, current, left_side=False, lower=True, transpose_a=True
    )
    half_solved = lax.linalg.triangular_solve(factor, rayleigh, left_side=True, lower=True)
    projected = lax.linalg.triangular_solve(
        factor, half_solved, left_side=False, lower=True, transpose_a=True
    )
    return (ortho_basis, projected)


def solution(mesh):
    in_specs = (
        P("row", "col", None, None),
        P("row", "col"),
        P(("row", "col")),
        P(("row", "col"), None),
        P(("row", "col"), None),
        P(),
        P(),
    )
    out_specs = (P(("row", "col"), None), P())
    return jax.shard_map(local, mesh=mesh, in_specs=in_specs, out_specs=out_specs, check_vma=False)
```

```python
import jax
import jax.numpy as jnp
from jax import lax
from jax.sharding import PartitionSpec as P

DEGREE = 4


def split_bf16(value):
    upper = value.astype(jnp.bfloat16)
    lower = (value - upper.astype(jnp.float32)).astype(jnp.bfloat16)
    return upper, lower


def split_dot(left, right_f32):
    upper, lower = split_bf16(right_f32)
    first = jnp.dot(left, upper, preferred_element_type=jnp.float32)
    return first + jnp.dot(left, lower, preferred_element_type=jnp.float32)


def butterfly_sum(value, axis):
    size = lax.axis_size(axis)
    if size & (size - 1):
        return lax.psum(value, axis)
    step = 1
    while step < size:
        pairs = [(index, index ^ step) for index in range(size)]
        value = value + lax.ppermute(value, axis, pairs)
        step *= 2
    return value


def all_sum(value):
    return butterfly_sum(butterfly_sum(value, "col"), "row")


def scatter_sum(value, axis):
    size = lax.axis_size(axis)
    here = lax.axis_index(axis)
    blocks = value.reshape(size, value.shape[0] // size, value.shape[1])
    total = jnp.take(blocks, here, axis=0)
    for shift in range(1, size):
        part = jnp.take(blocks, (here + shift) % size, axis=0)
        pairs = [(index, (index + shift) % size) for index in range(size)]
        total = total + lax.ppermute(part, axis, pairs)
    return total


def halving_scatter_sum(value, axis):
    size = lax.axis_size(axis)
    if size & (size - 1):
        return scatter_sum(value, axis)
    here = lax.axis_index(axis)
    rows = value.shape[0] // size
    blocks = value.reshape(size, rows, value.shape[1])
    step = 1
    while step < size:
        bit = (here // step) % 2
        paired = blocks.reshape(blocks.shape[0] // 2, 2, rows, value.shape[1])
        kept = lax.dynamic_index_in_dim(paired, bit, axis=1, keepdims=False)
        sent = lax.dynamic_index_in_dim(paired, 1 - bit, axis=1, keepdims=False)
        pairs = [(index, index ^ step) for index in range(size)]
        blocks = kept + lax.ppermute(sent, axis, pairs)
        step *= 2
    return blocks.reshape(rows, value.shape[1])


def doubling_gather(value, axis):
    size = lax.axis_size(axis)
    if size & (size - 1):
        return lax.all_gather(value, axis, axis=0, tiled=True)
    here = lax.axis_index(axis)
    result = value
    step = 1
    while step < size:
        pairs = [(index, index ^ step) for index in range(size)]
        other = lax.ppermute(result, axis, pairs)
        low = (here // step) % 2 == 0
        result = jnp.concatenate(
            [jnp.where(low, result, other), jnp.where(low, other, result)], axis=0
        )
        step *= 2
    return result


def direct_gather(value, axis):
    size = lax.axis_size(axis)
    here = lax.axis_index(axis)
    parts = [value]
    for shift in range(1, size):
        pairs = [(index, (index + shift) % size) for index in range(size)]
        parts.append(lax.ppermute(value, axis, pairs))
    stacked = jnp.stack(parts)
    order = (here - jnp.arange(size, dtype=jnp.int32)) % size
    return jnp.take(stacked, order, axis=0).reshape(-1, value.shape[1])


def exchange_gather(value, axis):
    size = lax.axis_size(axis)
    copies = jnp.broadcast_to(value[None], (size,) + value.shape)
    got = lax.all_to_all(copies, axis, 0, 0, tiled=False)
    return got.reshape(-1, value.shape[1])


def local(tiles, tile_cols, degree_scale, start_block, planted, strengths, bounds):
    piece_rows = start_block.shape[0]
    node_count = piece_rows * lax.axis_size("row") * lax.axis_size("col")
    tile_rows, slots, tile_size = tiles.shape[0], tiles.shape[1], tiles.shape[2]
    n_blocks = lax.axis_size("row") * piece_rows // tile_size
    weights = strengths[:, None]

    onehot = (tile_cols[:, :, None] == jnp.arange(n_blocks, dtype=jnp.int32)[None, None, :]).astype(jnp.bfloat16)
    dense = jnp.einsum("rst,rsab->ratb", onehot, tiles, preferred_element_type=jnp.float32)
    dense = dense.reshape(tile_rows * tile_size, n_blocks * tile_size)
    w_hi, w_lo = split_bf16(dense)

    planted_cols = doubling_gather(planted, "row")
    planted_rows = direct_gather(planted, "col")

    def operate(vector):
        scaled = (degree_scale[:, None] * vector).astype(jnp.bfloat16)
        gathered = exchange_gather(scaled, "row")
        product = jnp.dot(w_hi, gathered, preferred_element_type=jnp.float32)
        product = product + jnp.dot(w_lo, gathered, preferred_element_type=jnp.float32)
        partial = lax.dot_general(
            planted_cols, gathered, (((0,), (0,)), ((), ())), preferred_element_type=jnp.float32
        )
        product = product + split_dot(planted_rows, weights * partial) / node_count
        summed = halving_scatter_sum(product, "col")
        return degree_scale[:, None] * summed

    center = (bounds[1] + bounds[0]) * 0.5
    half_width = (bounds[1] - bounds[0]) * 0.5
    previous = start_block
    current = (operate(start_block) - center * start_block) / half_width
    for index_step in range(DEGREE - 1):
        applied = operate(current)
        following = 2.0 * (applied - center * current) / half_width - previous
        previous, current = (current, following)
    local_gram = jnp.dot(current.T, current, precision=lax.Precision.HIGHEST)
    applied = operate(current)
    local_rayleigh = jnp.dot(current.T, applied, precision=lax.Precision.HIGHEST)
    totals = all_sum(jnp.concatenate([local_gram, local_rayleigh], axis=0))
    gram_total, rayleigh_total = totals[: local_gram.shape[0]], totals[local_gram.shape[0] :]
    gram_matrix = gram_total / node_count
    rayleigh = rayleigh_total / node_count
    factor = jnp.linalg.cholesky(gram_matrix)
    ortho_basis = lax.linalg.triangular_solve(
        factor, current, left_side=False, lower=True, transpose_a=True
    )
    half_solved = lax.linalg.triangular_solve(factor, rayleigh, left_side=True, lower=True)
    projected = lax.linalg.triangular_solve(
        factor, half_solved, left_side=False, lower=True, transpose_a=True
    )
    return (ortho_basis, projected)


def solution(mesh):
    in_specs = (
        P("row", "col", None, None),
        P("row", "col"),
        P(("row", "col")),
        P(("row", "col"), None),
        P(("row", "col"), None),
        P(),
        P(),
    )
    out_specs = (P(("row", "col"), None), P())
    return jax.shard_map(local, mesh=mesh, in_specs=in_specs, out_specs=out_specs, check_vma=False)
```

```python
import jax
import jax.numpy as jnp
from jax import lax
from jax.sharding import PartitionSpec as P

DEGREE = 4


def split_bf16(value):
    upper = value.astype(jnp.bfloat16)
    lower = (value - upper.astype(jnp.float32)).astype(jnp.bfloat16)
    return upper, lower


def split_dot(left, right_f32):
    upper, lower = split_bf16(right_f32)
    first = jnp.dot(left, upper, preferred_element_type=jnp.float32)
    return first + jnp.dot(left, lower, preferred_element_type=jnp.float32)


def butterfly_sum(value, axis):
    size = lax.axis_size(axis)
    if size & (size - 1):
        return lax.psum(value, axis)
    step = 1
    while step < size:
        pairs = [(index, index ^ step) for index in range(size)]
        value = value + lax.ppermute(value, axis, pairs)
        step *= 2
    return value


def all_sum(value):
    return butterfly_sum(butterfly_sum(value, "col"), "row")


def scatter_sum(value, axis):
    size = lax.axis_size(axis)
    here = lax.axis_index(axis)
    blocks = value.reshape(size, value.shape[0] // size, value.shape[1])
    total = jnp.take(blocks, here, axis=0)
    for shift in range(1, size):
        part = jnp.take(blocks, (here + shift) % size, axis=0)
        pairs = [(index, (index + shift) % size) for index in range(size)]
        total = total + lax.ppermute(part, axis, pairs)
    return total


def halving_scatter_sum(value, axis):
    size = lax.axis_size(axis)
    if size & (size - 1):
        return scatter_sum(value, axis)
    here = lax.axis_index(axis)
    rows = value.shape[0] // size
    blocks = value.reshape(size, rows, value.shape[1])
    step = 1
    while step < size:
        bit = (here // step) % 2
        paired = blocks.reshape(blocks.shape[0] // 2, 2, rows, value.shape[1])
        kept = lax.dynamic_index_in_dim(paired, bit, axis=1, keepdims=False)
        sent = lax.dynamic_index_in_dim(paired, 1 - bit, axis=1, keepdims=False)
        pairs = [(index, index ^ step) for index in range(size)]
        blocks = kept + lax.ppermute(sent, axis, pairs)
        step *= 2
    return blocks.reshape(rows, value.shape[1])


def doubling_gather(value, axis):
    size = lax.axis_size(axis)
    if size & (size - 1):
        return lax.all_gather(value, axis, axis=0, tiled=True)
    here = lax.axis_index(axis)
    result = value
    step = 1
    while step < size:
        pairs = [(index, index ^ step) for index in range(size)]
        other = lax.ppermute(result, axis, pairs)
        low = (here // step) % 2 == 0
        result = jnp.concatenate(
            [jnp.where(low, result, other), jnp.where(low, other, result)], axis=0
        )
        step *= 2
    return result


def far_first_gather(value, axis):
    size = lax.axis_size(axis)
    if size & (size - 1):
        return lax.all_gather(value, axis, axis=0, tiled=True)
    here = lax.axis_index(axis)
    result = value[None]
    step = size // 2
    while step >= 1:
        pairs = [(index, index ^ step) for index in range(size)]
        other = lax.ppermute(result, axis, pairs)
        low = (here // step) % 2 == 0
        result = jnp.concatenate(
            [jnp.where(low, result, other), jnp.where(low, other, result)], axis=0
        )
        step //= 2
    bits = size.bit_length() - 1
    order = [int(format(index, f"0{bits}b")[::-1], 2) if bits else 0 for index in range(size)]
    return result[jnp.array(order)].reshape(-1, value.shape[1])


def local(tiles, tile_cols, degree_scale, start_block, planted, strengths, bounds):
    piece_rows = start_block.shape[0]
    node_count = piece_rows * lax.axis_size("row") * lax.axis_size("col")
    tile_rows, slots, tile_size = tiles.shape[0], tiles.shape[1], tiles.shape[2]
    n_blocks = lax.axis_size("row") * piece_rows // tile_size
    weights = strengths[:, None]

    onehot = (tile_cols[:, :, None] == jnp.arange(n_blocks, dtype=jnp.int32)[None, None, :]).astype(jnp.bfloat16)
    dense = jnp.einsum("rst,rsab->ratb", onehot, tiles, preferred_element_type=jnp.float32)
    dense = dense.reshape(tile_rows * tile_size, n_blocks * tile_size)
    w_hi, w_lo = split_bf16(dense)

    planted_cols = doubling_gather(planted, "row")
    planted_rows = far_first_gather(planted, "col")

    def operate(vector):
        scaled = (degree_scale[:, None] * vector).astype(jnp.bfloat16)
        gathered = doubling_gather(scaled, "row")
        product = jnp.dot(w_hi, gathered, preferred_element_type=jnp.float32)
        product = product + jnp.dot(w_lo, gathered, preferred_element_type=jnp.float32)
        partial = lax.dot_general(
            planted_cols, gathered, (((0,), (0,)), ((), ())), preferred_element_type=jnp.float32
        )
        product = product + split_dot(planted_rows, weights * partial) / node_count
        summed = halving_scatter_sum(product, "col")
        return degree_scale[:, None] * summed

    center = (bounds[1] + bounds[0]) * 0.5
    half_width = (bounds[1] - bounds[0]) * 0.5
    previous = start_block
    current = (operate(start_block) - center * start_block) / half_width
    for index_step in range(DEGREE - 1):
        applied = operate(current)
        following = 2.0 * (applied - center * current) / half_width - previous
        previous, current = (current, following)
    local_gram = jnp.dot(current.T, current, precision=lax.Precision.HIGHEST)
    applied = operate(current)
    local_rayleigh = jnp.dot(current.T, applied, precision=lax.Precision.HIGHEST)
    totals = all_sum(jnp.concatenate([local_gram, local_rayleigh], axis=0))
    gram_total, rayleigh_total = totals[: local_gram.shape[0]], totals[local_gram.shape[0] :]
    gram_matrix = gram_total / node_count
    rayleigh = rayleigh_total / node_count
    factor = jnp.linalg.cholesky(gram_matrix)
    ortho_basis = lax.linalg.triangular_solve(
        factor, current, left_side=False, lower=True, transpose_a=True
    )
    half_solved = lax.linalg.triangular_solve(factor, rayleigh, left_side=True, lower=True)
    projected = lax.linalg.triangular_solve(
        factor, half_solved, left_side=False, lower=True, transpose_a=True
    )
    return (ortho_basis, projected)


def solution(mesh):
    in_specs = (
        P("row", "col", None, None),
        P("row", "col"),
        P(("row", "col")),
        P(("row", "col"), None),
        P(("row", "col"), None),
        P(),
        P(),
    )
    out_specs = (P(("row", "col"), None), P())
    return jax.shard_map(local, mesh=mesh, in_specs=in_specs, out_specs=out_specs, check_vma=False)
```

```python
import jax
import jax.numpy as jnp
from jax import lax
from jax.experimental import pallas as pl
from jax.experimental.pallas import tpu as pltpu
from jax.sharding import PartitionSpec as P

DEGREE = 4


def split_bf16(value):
    upper = value.astype(jnp.bfloat16)
    lower = (value - upper.astype(jnp.float32)).astype(jnp.bfloat16)
    return upper, lower


def split_dot(left, right_f32):
    upper, lower = split_bf16(right_f32)
    first = jnp.dot(left, upper, preferred_element_type=jnp.float32)
    return first + jnp.dot(left, lower, preferred_element_type=jnp.float32)


def butterfly_sum(value, axis):
    size = lax.axis_size(axis)
    if size & (size - 1):
        return lax.psum(value, axis)
    step = 1
    while step < size:
        pairs = [(index, index ^ step) for index in range(size)]
        value = value + lax.ppermute(value, axis, pairs)
        step *= 2
    return value


def all_sum(value):
    return butterfly_sum(butterfly_sum(value, "col"), "row")


def scatter_sum(value, axis):
    size = lax.axis_size(axis)
    here = lax.axis_index(axis)
    blocks = value.reshape(size, value.shape[0] // size, value.shape[1])
    total = jnp.take(blocks, here, axis=0)
    for shift in range(1, size):
        part = jnp.take(blocks, (here + shift) % size, axis=0)
        pairs = [(index, (index + shift) % size) for index in range(size)]
        total = total + lax.ppermute(part, axis, pairs)
    return total


def halving_scatter_sum(value, axis):
    size = lax.axis_size(axis)
    if size & (size - 1):
        return scatter_sum(value, axis)
    here = lax.axis_index(axis)
    rows = value.shape[0] // size
    blocks = value.reshape(size, rows, value.shape[1])
    step = 1
    while step < size:
        bit = (here // step) % 2
        paired = blocks.reshape(blocks.shape[0] // 2, 2, rows, value.shape[1])
        kept = lax.dynamic_index_in_dim(paired, bit, axis=1, keepdims=False)
        sent = lax.dynamic_index_in_dim(paired, 1 - bit, axis=1, keepdims=False)
        pairs = [(index, index ^ step) for index in range(size)]
        blocks = kept + lax.ppermute(sent, axis, pairs)
        step *= 2
    return blocks.reshape(rows, value.shape[1])


def doubling_gather(value, axis):
    size = lax.axis_size(axis)
    if size & (size - 1):
        return lax.all_gather(value, axis, axis=0, tiled=True)
    here = lax.axis_index(axis)
    result = value
    step = 1
    while step < size:
        pairs = [(index, index ^ step) for index in range(size)]
        other = lax.ppermute(result, axis, pairs)
        low = (here // step) % 2 == 0
        result = jnp.concatenate(
            [jnp.where(low, result, other), jnp.where(low, other, result)], axis=0
        )
        step *= 2
    return result


def far_first_gather(value, axis):
    size = lax.axis_size(axis)
    if size & (size - 1):
        return lax.all_gather(value, axis, axis=0, tiled=True)
    here = lax.axis_index(axis)
    result = value[None]
    step = size // 2
    while step >= 1:
        pairs = [(index, index ^ step) for index in range(size)]
        other = lax.ppermute(result, axis, pairs)
        low = (here // step) % 2 == 0
        result = jnp.concatenate(
            [jnp.where(low, result, other), jnp.where(low, other, result)], axis=0
        )
        step //= 2
    bits = size.bit_length() - 1
    order = [int(format(index, f"0{bits}b")[::-1], 2) if bits else 0 for index in range(size)]
    return result[jnp.array(order)].reshape(-1, value.shape[1])


def dense_parts(tiles, tile_cols, n_blocks):
    tile_rows, slots, tile_size = tiles.shape[0], tiles.shape[1], tiles.shape[2]
    width = n_blocks * tile_size

    def kernel(cols_ref, tiles_ref, hi_ref, lo_ref, acc_ref):
        row = pl.program_id(0)
        acc_ref[...] = jnp.zeros_like(acc_ref)
        for slot in range(slots):
            start = pl.multiple_of(cols_ref[row, slot] * tile_size, tile_size)
            window = pl.ds(start, tile_size)
            acc_ref[:, window] = acc_ref[:, window] + tiles_ref[0, slot].astype(jnp.float32)
        total = acc_ref[...]
        upper = total.astype(jnp.bfloat16)
        hi_ref[...] = upper
        lo_ref[...] = (total - upper.astype(jnp.float32)).astype(jnp.bfloat16)

    grid_spec = pltpu.PrefetchScalarGridSpec(
        num_scalar_prefetch=1,
        grid=(tile_rows,),
        in_specs=[pl.BlockSpec((1, slots, tile_size, tile_size), lambda r, cols: (r, 0, 0, 0))],
        out_specs=[
            pl.BlockSpec((tile_size, width), lambda r, cols: (r, 0)),
            pl.BlockSpec((tile_size, width), lambda r, cols: (r, 0)),
        ],
        scratch_shapes=[pltpu.VMEM((tile_size, width), jnp.float32)],
    )
    shape = jax.ShapeDtypeStruct((tile_rows * tile_size, width), jnp.bfloat16)
    return pl.pallas_call(
        kernel,
        grid_spec=grid_spec,
        out_shape=(shape, shape),
        compiler_params=pltpu.CompilerParams(dimension_semantics=("arbitrary",)),
    )(tile_cols, tiles)


def local(tiles, tile_cols, degree_scale, start_block, planted, strengths, bounds):
    piece_rows = start_block.shape[0]
    node_count = piece_rows * lax.axis_size("row") * lax.axis_size("col")
    tile_rows, slots, tile_size = tiles.shape[0], tiles.shape[1], tiles.shape[2]
    n_blocks = lax.axis_size("row") * piece_rows // tile_size
    weights = strengths[:, None]

    w_hi, w_lo = dense_parts(tiles, tile_cols, n_blocks)

    planted_cols = doubling_gather(planted, "row")
    planted_rows = far_first_gather(planted, "col")

    def operate(vector):
        scaled = (degree_scale[:, None] * vector).astype(jnp.bfloat16)
        gathered = doubling_gather(scaled, "row")
        product = jnp.dot(w_hi, gathered, preferred_element_type=jnp.float32)
        product = product + jnp.dot(w_lo, gathered, preferred_element_type=jnp.float32)
        partial = lax.dot_general(
            planted_cols, gathered, (((0,), (0,)), ((), ())), preferred_element_type=jnp.float32
        )
        product = product + split_dot(planted_rows, weights * partial) / node_count
        summed = halving_scatter_sum(product, "col")
        return degree_scale[:, None] * summed

    center = (bounds[1] + bounds[0]) * 0.5
    half_width = (bounds[1] - bounds[0]) * 0.5
    previous = start_block
    current = (operate(start_block) - center * start_block) / half_width
    for index_step in range(DEGREE - 1):
        applied = operate(current)
        following = 2.0 * (applied - center * current) / half_width - previous
        previous, current = (current, following)
    local_gram = jnp.dot(current.T, current, precision=lax.Precision.HIGHEST)
    applied = operate(current)
    local_rayleigh = jnp.dot(current.T, applied, precision=lax.Precision.HIGHEST)
    totals = all_sum(jnp.concatenate([local_gram, local_rayleigh], axis=0))
    gram_total, rayleigh_total = totals[: local_gram.shape[0]], totals[local_gram.shape[0] :]
    gram_matrix = gram_total / node_count
    rayleigh = rayleigh_total / node_count
    factor = jnp.linalg.cholesky(gram_matrix)
    ortho_basis = lax.linalg.triangular_solve(
        factor, current, left_side=False, lower=True, transpose_a=True
    )
    half_solved = lax.linalg.triangular_solve(factor, rayleigh, left_side=True, lower=True)
    projected = lax.linalg.triangular_solve(
        factor, half_solved, left_side=False, lower=True, transpose_a=True
    )
    return (ortho_basis, projected)


def solution(mesh):
    in_specs = (
        P("row", "col", None, None),
        P("row", "col"),
        P(("row", "col")),
        P(("row", "col"), None),
        P(("row", "col"), None),
        P(),
        P(),
    )
    out_specs = (P(("row", "col"), None), P())
    return jax.shard_map(local, mesh=mesh, in_specs=in_specs, out_specs=out_specs, check_vma=False)
```

```python
import jax
import jax.numpy as jnp
from jax import lax
from jax.sharding import PartitionSpec as P

DEGREE = 4


def split_bf16(value):
    upper = value.astype(jnp.bfloat16)
    lower = (value - upper.astype(jnp.float32)).astype(jnp.bfloat16)
    return upper, lower


def split_dot(left, right_f32):
    upper, lower = split_bf16(right_f32)
    first = jnp.dot(left, upper, preferred_element_type=jnp.float32)
    return first + jnp.dot(left, lower, preferred_element_type=jnp.float32)


def butterfly_sum(value, axis):
    size = lax.axis_size(axis)
    if size & (size - 1):
        return lax.psum(value, axis)
    step = 1
    while step < size:
        pairs = [(index, index ^ step) for index in range(size)]
        value = value + lax.ppermute(value, axis, pairs)
        step *= 2
    return value


def all_sum(value):
    return butterfly_sum(butterfly_sum(value, "col"), "row")


def scatter_sum(value, axis):
    size = lax.axis_size(axis)
    here = lax.axis_index(axis)
    blocks = value.reshape(size, value.shape[0] // size, value.shape[1])
    total = jnp.take(blocks, here, axis=0)
    for shift in range(1, size):
        part = jnp.take(blocks, (here + shift) % size, axis=0)
        pairs = [(index, (index + shift) % size) for index in range(size)]
        total = total + lax.ppermute(part, axis, pairs)
    return total


def halving_scatter_sum(value, axis):
    size = lax.axis_size(axis)
    if size & (size - 1):
        return scatter_sum(value, axis)
    here = lax.axis_index(axis)
    rows = value.shape[0] // size
    blocks = value.reshape(size, rows, value.shape[1])
    step = 1
    while step < size:
        bit = (here // step) % 2
        paired = blocks.reshape(blocks.shape[0] // 2, 2, rows, value.shape[1])
        kept = lax.dynamic_index_in_dim(paired, bit, axis=1, keepdims=False)
        sent = lax.dynamic_index_in_dim(paired, 1 - bit, axis=1, keepdims=False)
        pairs = [(index, index ^ step) for index in range(size)]
        blocks = kept + lax.ppermute(sent, axis, pairs)
        step *= 2
    return blocks.reshape(rows, value.shape[1])


def doubling_gather(value, axis):
    size = lax.axis_size(axis)
    if size & (size - 1):
        return lax.all_gather(value, axis, axis=0, tiled=True)
    here = lax.axis_index(axis)
    result = value
    step = 1
    while step < size:
        pairs = [(index, index ^ step) for index in range(size)]
        other = lax.ppermute(result, axis, pairs)
        low = (here // step) % 2 == 0
        result = jnp.concatenate(
            [jnp.where(low, result, other), jnp.where(low, other, result)], axis=0
        )
        step *= 2
    return result


def far_first_gather(value, axis):
    size = lax.axis_size(axis)
    if size & (size - 1):
        return lax.all_gather(value, axis, axis=0, tiled=True)
    here = lax.axis_index(axis)
    result = value[None]
    step = size // 2
    while step >= 1:
        pairs = [(index, index ^ step) for index in range(size)]
        other = lax.ppermute(result, axis, pairs)
        low = (here // step) % 2 == 0
        result = jnp.concatenate(
            [jnp.where(low, result, other), jnp.where(low, other, result)], axis=0
        )
        step //= 2
    bits = size.bit_length() - 1
    order = [int(format(index, f"0{bits}b")[::-1], 2) if bits else 0 for index in range(size)]
    return result[jnp.array(order)].reshape(-1, value.shape[1])


def gather_segments(value, axis):
    size = lax.axis_size(axis)
    here = lax.axis_index(axis)
    segments = [value]
    result = value
    step = 1
    while step < size:
        pairs = [(index, index ^ step) for index in range(size)]
        other = lax.ppermute(result, axis, pairs)
        segments.append(other)
        if step * 2 < size:
            low = (here // step) % 2 == 0
            result = jnp.concatenate(
                [jnp.where(low, result, other), jnp.where(low, other, result)], axis=0
            )
        step *= 2
    return segments


def segment_pieces(axis):
    size = lax.axis_size(axis)
    here = lax.axis_index(axis)
    pieces = [here[None]]
    step = 1
    while step < size:
        start = ((here ^ step) // step) * step
        pieces.append(start + jnp.arange(step, dtype=jnp.int32))
        step *= 2
    return jnp.concatenate(pieces).astype(jnp.int32)


def local(tiles, tile_cols, degree_scale, start_block, planted, strengths, bounds):
    piece_rows = start_block.shape[0]
    node_count = piece_rows * lax.axis_size("row") * lax.axis_size("col")
    tile_rows, slots, tile_size = tiles.shape[0], tiles.shape[1], tiles.shape[2]
    n_blocks = lax.axis_size("row") * piece_rows // tile_size
    weights = strengths[:, None]

    row_size = lax.axis_size("row")
    in_order = row_size & (row_size - 1) == 0
    per_piece = piece_rows // tile_size
    if in_order:
        pieces = segment_pieces("row")
        block_order = (pieces[:, None] * per_piece + jnp.arange(per_piece, dtype=jnp.int32)[None, :]).reshape(-1)
    else:
        block_order = jnp.arange(n_blocks, dtype=jnp.int32)

    onehot = (tile_cols[:, :, None] == block_order[None, None, :]).astype(jnp.bfloat16)
    dense = jnp.einsum("rst,rsab->ratb", onehot, tiles, preferred_element_type=jnp.float32)
    dense = dense.reshape(tile_rows * tile_size, n_blocks * tile_size)
    w_hi, w_lo = split_bf16(dense)

    if in_order:
        planted_segments = gather_segments(planted, "row")
    else:
        planted_segments = [lax.all_gather(planted, "row", axis=0, tiled=True)]
    planted_rows = far_first_gather(planted, "col")

    def operate(vector):
        scaled = (degree_scale[:, None] * vector).astype(jnp.bfloat16)
        if in_order:
            segments = gather_segments(scaled, "row")
        else:
            segments = [lax.all_gather(scaled, "row", axis=0, tiled=True)]
        product = None
        partial = None
        offset = 0
        for segment, planted_part in zip(segments, planted_segments):
            columns = slice(offset, offset + segment.shape[0])
            offset += segment.shape[0]
            piece = jnp.dot(w_hi[:, columns], segment, preferred_element_type=jnp.float32)
            piece = piece + jnp.dot(w_lo[:, columns], segment, preferred_element_type=jnp.float32)
            inner = lax.dot_general(
                planted_part, segment, (((0,), (0,)), ((), ())), preferred_element_type=jnp.float32
            )
            product = piece if product is None else product + piece
            partial = inner if partial is None else partial + inner
        product = product + split_dot(planted_rows, weights * partial) / node_count
        summed = halving_scatter_sum(product, "col")
        return degree_scale[:, None] * summed

    center = (bounds[1] + bounds[0]) * 0.5
    half_width = (bounds[1] - bounds[0]) * 0.5
    previous = start_block
    current = (operate(start_block) - center * start_block) / half_width
    for index_step in range(DEGREE - 1):
        applied = operate(current)
        following = 2.0 * (applied - center * current) / half_width - previous
        previous, current = (current, following)
    local_gram = jnp.dot(current.T, current, precision=lax.Precision.HIGHEST)
    applied = operate(current)
    local_rayleigh = jnp.dot(current.T, applied, precision=lax.Precision.HIGHEST)
    totals = all_sum(jnp.concatenate([local_gram, local_rayleigh], axis=0))
    gram_total, rayleigh_total = totals[: local_gram.shape[0]], totals[local_gram.shape[0] :]
    gram_matrix = gram_total / node_count
    rayleigh = rayleigh_total / node_count
    factor = jnp.linalg.cholesky(gram_matrix)
    ortho_basis = lax.linalg.triangular_solve(
        factor, current, left_side=False, lower=True, transpose_a=True
    )
    half_solved = lax.linalg.triangular_solve(factor, rayleigh, left_side=True, lower=True)
    projected = lax.linalg.triangular_solve(
        factor, half_solved, left_side=False, lower=True, transpose_a=True
    )
    return (ortho_basis, projected)


def solution(mesh):
    in_specs = (
        P("row", "col", None, None),
        P("row", "col"),
        P(("row", "col")),
        P(("row", "col"), None),
        P(("row", "col"), None),
        P(),
        P(),
    )
    out_specs = (P(("row", "col"), None), P())
    return jax.shard_map(local, mesh=mesh, in_specs=in_specs, out_specs=out_specs, check_vma=False)
```

```python
import jax
import jax.numpy as jnp
from jax import lax
from jax.sharding import PartitionSpec as P

DEGREE = 4


def split_bf16(value):
    upper = value.astype(jnp.bfloat16)
    lower = (value - upper.astype(jnp.float32)).astype(jnp.bfloat16)
    return upper, lower


def split_dot(left, right_f32):
    upper, lower = split_bf16(right_f32)
    first = jnp.dot(left, upper, preferred_element_type=jnp.float32)
    return first + jnp.dot(left, lower, preferred_element_type=jnp.float32)


def butterfly_sum(value, axis):
    size = lax.axis_size(axis)
    if size & (size - 1):
        return lax.psum(value, axis)
    step = 1
    while step < size:
        pairs = [(index, index ^ step) for index in range(size)]
        value = value + lax.ppermute(value, axis, pairs)
        step *= 2
    return value


def all_sum(value):
    return butterfly_sum(butterfly_sum(value, "col"), "row")


def scatter_sum(value, axis):
    size = lax.axis_size(axis)
    here = lax.axis_index(axis)
    blocks = value.reshape(size, value.shape[0] // size, value.shape[1])
    total = jnp.take(blocks, here, axis=0)
    for shift in range(1, size):
        part = jnp.take(blocks, (here + shift) % size, axis=0)
        pairs = [(index, (index + shift) % size) for index in range(size)]
        total = total + lax.ppermute(part, axis, pairs)
    return total


def halving_scatter_sum(value, axis):
    size = lax.axis_size(axis)
    if size & (size - 1):
        return scatter_sum(value, axis)
    here = lax.axis_index(axis)
    rows = value.shape[0] // size
    blocks = value.reshape(size, rows, value.shape[1])
    step = 1
    while step < size:
        bit = (here // step) % 2
        paired = blocks.reshape(blocks.shape[0] // 2, 2, rows, value.shape[1])
        kept = lax.dynamic_index_in_dim(paired, bit, axis=1, keepdims=False)
        sent = lax.dynamic_index_in_dim(paired, 1 - bit, axis=1, keepdims=False)
        pairs = [(index, index ^ step) for index in range(size)]
        blocks = kept + lax.ppermute(sent, axis, pairs)
        step *= 2
    return blocks.reshape(rows, value.shape[1])


def doubling_gather(value, axis):
    size = lax.axis_size(axis)
    if size & (size - 1):
        return lax.all_gather(value, axis, axis=0, tiled=True)
    here = lax.axis_index(axis)
    result = value
    step = 1
    while step < size:
        pairs = [(index, index ^ step) for index in range(size)]
        other = lax.ppermute(result, axis, pairs)
        low = (here // step) % 2 == 0
        result = jnp.concatenate(
            [jnp.where(low, result, other), jnp.where(low, other, result)], axis=0
        )
        step *= 2
    return result


def far_first_gather(value, axis):
    size = lax.axis_size(axis)
    if size & (size - 1):
        return lax.all_gather(value, axis, axis=0, tiled=True)
    here = lax.axis_index(axis)
    result = value[None]
    step = size // 2
    while step >= 1:
        pairs = [(index, index ^ step) for index in range(size)]
        other = lax.ppermute(result, axis, pairs)
        low = (here // step) % 2 == 0
        result = jnp.concatenate(
            [jnp.where(low, result, other), jnp.where(low, other, result)], axis=0
        )
        step //= 2
    bits = size.bit_length() - 1
    order = [int(format(index, f"0{bits}b")[::-1], 2) if bits else 0 for index in range(size)]
    return result[jnp.array(order)].reshape(-1, value.shape[1])


def gather_segments(value, axis):
    size = lax.axis_size(axis)
    here = lax.axis_index(axis)
    segments = [value]
    result = value
    step = 1
    while step < size:
        pairs = [(index, index ^ step) for index in range(size)]
        other = lax.ppermute(result, axis, pairs)
        segments.append(other)
        if step * 2 < size:
            low = (here // step) % 2 == 0
            result = jnp.concatenate(
                [jnp.where(low, result, other), jnp.where(low, other, result)], axis=0
            )
        step *= 2
    return segments


def segment_pieces(axis):
    size = lax.axis_size(axis)
    here = lax.axis_index(axis)
    pieces = [here[None]]
    step = 1
    while step < size:
        start = ((here ^ step) // step) * step
        pieces.append(start + jnp.arange(step, dtype=jnp.int32))
        step *= 2
    return jnp.concatenate(pieces).astype(jnp.int32)


def local(tiles, tile_cols, degree_scale, start_block, planted, strengths, bounds):
    piece_rows = start_block.shape[0]
    node_count = piece_rows * lax.axis_size("row") * lax.axis_size("col")
    tile_rows, slots, tile_size = tiles.shape[0], tiles.shape[1], tiles.shape[2]
    n_blocks = lax.axis_size("row") * piece_rows // tile_size
    weights = strengths[:, None]

    row_size = lax.axis_size("row")
    in_order = row_size & (row_size - 1) == 0
    per_piece = piece_rows // tile_size
    if in_order:
        pieces = segment_pieces("row")
        block_order = (pieces[:, None] * per_piece + jnp.arange(per_piece, dtype=jnp.int32)[None, :]).reshape(-1)
        arrival = jnp.argsort(block_order).astype(jnp.int32)[tile_cols]
    else:
        arrival = tile_cols

    onehot = (arrival[:, :, None] == jnp.arange(n_blocks, dtype=jnp.int32)[None, None, :]).astype(jnp.bfloat16)
    dense = jnp.einsum("rst,rsab->ratb", onehot, tiles, preferred_element_type=jnp.float32)
    dense = dense.reshape(tile_rows * tile_size, n_blocks * tile_size)
    w_hi, w_lo = split_bf16(dense)

    if in_order:
        planted_segments = gather_segments(planted, "row")
    else:
        planted_segments = [lax.all_gather(planted, "row", axis=0, tiled=True)]
    planted_rows = far_first_gather(planted, "col")

    def operate(vector):
        scaled = (degree_scale[:, None] * vector).astype(jnp.bfloat16)
        if in_order:
            segments = gather_segments(scaled, "row")
        else:
            segments = [lax.all_gather(scaled, "row", axis=0, tiled=True)]
        product = None
        partial = None
        offset = 0
        for segment, planted_part in zip(segments, planted_segments):
            columns = slice(offset, offset + segment.shape[0])
            offset += segment.shape[0]
            piece = jnp.dot(w_hi[:, columns], segment, preferred_element_type=jnp.float32)
            piece = piece + jnp.dot(w_lo[:, columns], segment, preferred_element_type=jnp.float32)
            inner = lax.dot_general(
                planted_part, segment, (((0,), (0,)), ((), ())), preferred_element_type=jnp.float32
            )
            product = piece if product is None else product + piece
            partial = inner if partial is None else partial + inner
        product = product + split_dot(planted_rows, weights * partial) / node_count
        summed = halving_scatter_sum(product, "col")
        return degree_scale[:, None] * summed

    center = (bounds[1] + bounds[0]) * 0.5
    half_width = (bounds[1] - bounds[0]) * 0.5
    previous = start_block
    current = (operate(start_block) - center * start_block) / half_width
    for index_step in range(DEGREE - 1):
        applied = operate(current)
        following = 2.0 * (applied - center * current) / half_width - previous
        previous, current = (current, following)
    local_gram = jnp.dot(current.T, current, precision=lax.Precision.HIGHEST)
    applied = operate(current)
    local_rayleigh = jnp.dot(current.T, applied, precision=lax.Precision.HIGHEST)
    totals = all_sum(jnp.concatenate([local_gram, local_rayleigh], axis=0))
    gram_total, rayleigh_total = totals[: local_gram.shape[0]], totals[local_gram.shape[0] :]
    gram_matrix = gram_total / node_count
    rayleigh = rayleigh_total / node_count
    factor = jnp.linalg.cholesky(gram_matrix)
    ortho_basis = lax.linalg.triangular_solve(
        factor, current, left_side=False, lower=True, transpose_a=True
    )
    half_solved = lax.linalg.triangular_solve(factor, rayleigh, left_side=True, lower=True)
    projected = lax.linalg.triangular_solve(
        factor, half_solved, left_side=False, lower=True, transpose_a=True
    )
    return (ortho_basis, projected)


def solution(mesh):
    in_specs = (
        P("row", "col", None, None),
        P("row", "col"),
        P(("row", "col")),
        P(("row", "col"), None),
        P(("row", "col"), None),
        P(),
        P(),
    )
    out_specs = (P(("row", "col"), None), P())
    return jax.shard_map(local, mesh=mesh, in_specs=in_specs, out_specs=out_specs, check_vma=False)
```

```python
import jax
import jax.numpy as jnp
from jax import lax
from jax.sharding import PartitionSpec as P

DEGREE = 4


def split_bf16(value):
    upper = value.astype(jnp.bfloat16)
    lower = (value - upper.astype(jnp.float32)).astype(jnp.bfloat16)
    return upper, lower


def split_dot(left, right_f32):
    upper, lower = split_bf16(right_f32)
    first = jnp.dot(left, upper, preferred_element_type=jnp.float32)
    return first + jnp.dot(left, lower, preferred_element_type=jnp.float32)


def butterfly_sum(value, axis):
    size = lax.axis_size(axis)
    if size & (size - 1):
        return lax.psum(value, axis)
    step = 1
    while step < size:
        pairs = [(index, index ^ step) for index in range(size)]
        value = value + lax.ppermute(value, axis, pairs)
        step *= 2
    return value


def all_sum(value):
    return butterfly_sum(butterfly_sum(value, "col"), "row")


def scatter_sum(value, axis):
    size = lax.axis_size(axis)
    here = lax.axis_index(axis)
    blocks = value.reshape(size, value.shape[0] // size, value.shape[1])
    total = jnp.take(blocks, here, axis=0)
    for shift in range(1, size):
        part = jnp.take(blocks, (here + shift) % size, axis=0)
        pairs = [(index, (index + shift) % size) for index in range(size)]
        total = total + lax.ppermute(part, axis, pairs)
    return total


def halving_scatter_sum(value, axis):
    size = lax.axis_size(axis)
    if size & (size - 1):
        return scatter_sum(value, axis)
    here = lax.axis_index(axis)
    rows = value.shape[0] // size
    blocks = value.reshape(size, rows, value.shape[1])
    step = 1
    while step < size:
        bit = (here // step) % 2
        paired = blocks.reshape(blocks.shape[0] // 2, 2, rows, value.shape[1])
        kept = lax.dynamic_index_in_dim(paired, bit, axis=1, keepdims=False)
        sent = lax.dynamic_index_in_dim(paired, 1 - bit, axis=1, keepdims=False)
        pairs = [(index, index ^ step) for index in range(size)]
        blocks = kept + lax.ppermute(sent, axis, pairs)
        step *= 2
    return blocks.reshape(rows, value.shape[1])


def doubling_gather(value, axis):
    size = lax.axis_size(axis)
    if size & (size - 1):
        return lax.all_gather(value, axis, axis=0, tiled=True)
    here = lax.axis_index(axis)
    result = value
    step = 1
    while step < size:
        pairs = [(index, index ^ step) for index in range(size)]
        other = lax.ppermute(result, axis, pairs)
        low = (here // step) % 2 == 0
        result = jnp.concatenate(
            [jnp.where(low, result, other), jnp.where(low, other, result)], axis=0
        )
        step *= 2
    return result


def far_first_gather(value, axis):
    size = lax.axis_size(axis)
    if size & (size - 1):
        return lax.all_gather(value, axis, axis=0, tiled=True)
    here = lax.axis_index(axis)
    result = value[None]
    step = size // 2
    while step >= 1:
        pairs = [(index, index ^ step) for index in range(size)]
        other = lax.ppermute(result, axis, pairs)
        low = (here // step) % 2 == 0
        result = jnp.concatenate(
            [jnp.where(low, result, other), jnp.where(low, other, result)], axis=0
        )
        step //= 2
    bits = size.bit_length() - 1
    order = [int(format(index, f"0{bits}b")[::-1], 2) if bits else 0 for index in range(size)]
    return result[jnp.array(order)].reshape(-1, value.shape[1])


def split_scatter_sum(kept, sent, axis):
    size = lax.axis_size(axis)
    here = lax.axis_index(axis)
    rows, width = kept.shape[0] // (size // 2), kept.shape[1]
    blocks = kept.reshape(size // 2, rows, width)
    blocks = blocks + lax.ppermute(sent.reshape(size // 2, rows, width), axis, [(i, i ^ 1) for i in range(size)])
    step = 2
    while step < size:
        bit = (here // step) % 2
        paired = blocks.reshape(blocks.shape[0] // 2, 2, rows, width)
        kept_part = lax.dynamic_index_in_dim(paired, bit, axis=1, keepdims=False)
        sent_part = lax.dynamic_index_in_dim(paired, 1 - bit, axis=1, keepdims=False)
        pairs = [(index, index ^ step) for index in range(size)]
        blocks = kept_part + lax.ppermute(sent_part, axis, pairs)
        step *= 2
    return blocks.reshape(rows, width)


def local(tiles, tile_cols, degree_scale, start_block, planted, strengths, bounds):
    piece_rows = start_block.shape[0]
    node_count = piece_rows * lax.axis_size("row") * lax.axis_size("col")
    tile_rows, slots, tile_size = tiles.shape[0], tiles.shape[1], tiles.shape[2]
    n_blocks = lax.axis_size("row") * piece_rows // tile_size
    weights = strengths[:, None]

    onehot = (tile_cols[:, :, None] == jnp.arange(n_blocks, dtype=jnp.int32)[None, None, :]).astype(jnp.bfloat16)
    dense = jnp.einsum("rst,rsab->ratb", onehot, tiles, preferred_element_type=jnp.float32)
    dense = dense.reshape(tile_rows * tile_size, n_blocks * tile_size)
    col_size = lax.axis_size("col")
    split_rows = col_size % 2 == 0 and col_size & (col_size - 1) == 0
    if split_rows:
        col_bit = lax.axis_index("col") % 2
        halves = jnp.arange(col_size // 2, dtype=jnp.int32) * 2
        block_perm = jnp.concatenate([halves + col_bit, halves + 1 - col_bit])
        dense = jnp.take(dense.reshape(col_size, -1, dense.shape[1]), block_perm, axis=0).reshape(dense.shape)
    w_hi, w_lo = split_bf16(dense)

    planted_cols = doubling_gather(planted, "row")
    planted_rows = far_first_gather(planted, "col")
    if split_rows:
        planted_rows = jnp.take(
            planted_rows.reshape(col_size, -1, planted_rows.shape[1]), block_perm, axis=0
        ).reshape(planted_rows.shape)

    def operate(vector):
        scaled = (degree_scale[:, None] * vector).astype(jnp.bfloat16)
        gathered = doubling_gather(scaled, "row")
        partial = lax.dot_general(
            planted_cols, gathered, (((0,), (0,)), ((), ())), preferred_element_type=jnp.float32
        )
        lift = weights * partial

        def rows_product(part):
            product = jnp.dot(w_hi[part], gathered, preferred_element_type=jnp.float32)
            product = product + jnp.dot(w_lo[part], gathered, preferred_element_type=jnp.float32)
            return product + split_dot(planted_rows[part], lift) / node_count

        if split_rows:
            middle = w_hi.shape[0] // 2
            sent = rows_product(slice(middle, None))
            kept = rows_product(slice(0, middle))
            summed = split_scatter_sum(kept, sent, "col")
        else:
            summed = halving_scatter_sum(rows_product(slice(None)), "col")
        return degree_scale[:, None] * summed

    center = (bounds[1] + bounds[0]) * 0.5
    half_width = (bounds[1] - bounds[0]) * 0.5
    previous = start_block
    current = (operate(start_block) - center * start_block) / half_width
    for index_step in range(DEGREE - 1):
        applied = operate(current)
        following = 2.0 * (applied - center * current) / half_width - previous
        previous, current = (current, following)
    local_gram = jnp.dot(current.T, current, precision=lax.Precision.HIGHEST)
    applied = operate(current)
    local_rayleigh = jnp.dot(current.T, applied, precision=lax.Precision.HIGHEST)
    totals = all_sum(jnp.concatenate([local_gram, local_rayleigh], axis=0))
    gram_total, rayleigh_total = totals[: local_gram.shape[0]], totals[local_gram.shape[0] :]
    gram_matrix = gram_total / node_count
    rayleigh = rayleigh_total / node_count
    factor = jnp.linalg.cholesky(gram_matrix)
    ortho_basis = lax.linalg.triangular_solve(
        factor, current, left_side=False, lower=True, transpose_a=True
    )
    half_solved = lax.linalg.triangular_solve(factor, rayleigh, left_side=True, lower=True)
    projected = lax.linalg.triangular_solve(
        factor, half_solved, left_side=False, lower=True, transpose_a=True
    )
    return (ortho_basis, projected)


def solution(mesh):
    in_specs = (
        P("row", "col", None, None),
        P("row", "col"),
        P(("row", "col")),
        P(("row", "col"), None),
        P(("row", "col"), None),
        P(),
        P(),
    )
    out_specs = (P(("row", "col"), None), P())
    return jax.shard_map(local, mesh=mesh, in_specs=in_specs, out_specs=out_specs, check_vma=False)
```

```python
import jax
import jax.numpy as jnp
from jax import lax
from jax.sharding import PartitionSpec as P

DEGREE = 4


def split_bf16(value):
    upper = value.astype(jnp.bfloat16)
    lower = (value - upper.astype(jnp.float32)).astype(jnp.bfloat16)
    return upper, lower


def split_dot(left, right_f32):
    upper, lower = split_bf16(right_f32)
    first = jnp.dot(left, upper, preferred_element_type=jnp.float32)
    return first + jnp.dot(left, lower, preferred_element_type=jnp.float32)


def butterfly_sum(value, axis):
    size = lax.axis_size(axis)
    if size & (size - 1):
        return lax.psum(value, axis)
    step = 1
    while step < size:
        pairs = [(index, index ^ step) for index in range(size)]
        value = value + lax.ppermute(value, axis, pairs)
        step *= 2
    return value


def all_sum(value):
    return butterfly_sum(butterfly_sum(value, "col"), "row")


def scatter_sum(value, axis):
    size = lax.axis_size(axis)
    here = lax.axis_index(axis)
    blocks = value.reshape(size, value.shape[0] // size, value.shape[1])
    total = jnp.take(blocks, here, axis=0)
    for shift in range(1, size):
        part = jnp.take(blocks, (here + shift) % size, axis=0)
        pairs = [(index, (index + shift) % size) for index in range(size)]
        total = total + lax.ppermute(part, axis, pairs)
    return total


def halving_scatter_sum(value, axis):
    size = lax.axis_size(axis)
    if size & (size - 1):
        return scatter_sum(value, axis)
    here = lax.axis_index(axis)
    rows = value.shape[0] // size
    blocks = value.reshape(size, rows, value.shape[1])
    step = 1
    while step < size:
        bit = (here // step) % 2
        paired = blocks.reshape(blocks.shape[0] // 2, 2, rows, value.shape[1])
        kept = lax.dynamic_index_in_dim(paired, bit, axis=1, keepdims=False)
        sent = lax.dynamic_index_in_dim(paired, 1 - bit, axis=1, keepdims=False)
        pairs = [(index, index ^ step) for index in range(size)]
        blocks = kept + lax.ppermute(sent, axis, pairs)
        step *= 2
    return blocks.reshape(rows, value.shape[1])


def doubling_gather(value, axis):
    size = lax.axis_size(axis)
    if size & (size - 1):
        return lax.all_gather(value, axis, axis=0, tiled=True)
    here = lax.axis_index(axis)
    result = value
    step = 1
    while step < size:
        pairs = [(index, index ^ step) for index in range(size)]
        other = lax.ppermute(result, axis, pairs)
        low = (here // step) % 2 == 0
        result = jnp.concatenate(
            [jnp.where(low, result, other), jnp.where(low, other, result)], axis=0
        )
        step *= 2
    return result


def far_first_gather(value, axis):
    size = lax.axis_size(axis)
    if size & (size - 1):
        return lax.all_gather(value, axis, axis=0, tiled=True)
    here = lax.axis_index(axis)
    result = value[None]
    step = size // 2
    while step >= 1:
        pairs = [(index, index ^ step) for index in range(size)]
        other = lax.ppermute(result, axis, pairs)
        low = (here // step) % 2 == 0
        result = jnp.concatenate(
            [jnp.where(low, result, other), jnp.where(low, other, result)], axis=0
        )
        step //= 2
    bits = size.bit_length() - 1
    result = result.reshape((2,) * bits + value.shape)
    result = jnp.transpose(result, tuple(reversed(range(bits))) + (bits, bits + 1))
    return result.reshape(-1, value.shape[1])


def local(tiles, tile_cols, degree_scale, start_block, planted, strengths, bounds):
    piece_rows = start_block.shape[0]
    node_count = piece_rows * lax.axis_size("row") * lax.axis_size("col")
    tile_rows, slots, tile_size = tiles.shape[0], tiles.shape[1], tiles.shape[2]
    n_blocks = lax.axis_size("row") * piece_rows // tile_size
    weights = strengths[:, None]

    onehot = (tile_cols[:, :, None] == jnp.arange(n_blocks, dtype=jnp.int32)[None, None, :]).astype(jnp.bfloat16)
    dense = jnp.einsum("rst,rsab->ratb", onehot, tiles, preferred_element_type=jnp.float32)
    dense = dense.reshape(tile_rows * tile_size, n_blocks * tile_size)
    w_hi, w_lo = split_bf16(dense)

    planted_cols = doubling_gather(planted, "row")
    planted_rows = far_first_gather(planted, "col")

    def operate(vector):
        scaled = (degree_scale[:, None] * vector).astype(jnp.bfloat16)
        gathered = doubling_gather(scaled, "row")
        product = jnp.dot(w_hi, gathered, preferred_element_type=jnp.float32)
        product = product + jnp.dot(w_lo, gathered, preferred_element_type=jnp.float32)
        partial = lax.dot_general(
            planted_cols, gathered, (((0,), (0,)), ((), ())), preferred_element_type=jnp.float32
        )
        product = product + split_dot(planted_rows, weights * partial) / node_count
        summed = halving_scatter_sum(product, "col")
        return degree_scale[:, None] * summed

    center = (bounds[1] + bounds[0]) * 0.5
    half_width = (bounds[1] - bounds[0]) * 0.5
    previous = start_block
    current = (operate(start_block) - center * start_block) / half_width
    for index_step in range(DEGREE - 1):
        applied = operate(current)
        following = 2.0 * (applied - center * current) / half_width - previous
        previous, current = (current, following)
    local_gram = jnp.dot(current.T, current, precision=lax.Precision.HIGHEST)
    applied = operate(current)
    local_rayleigh = jnp.dot(current.T, applied, precision=lax.Precision.HIGHEST)
    totals = all_sum(jnp.concatenate([local_gram, local_rayleigh], axis=0))
    gram_total, rayleigh_total = totals[: local_gram.shape[0]], totals[local_gram.shape[0] :]
    gram_matrix = gram_total / node_count
    rayleigh = rayleigh_total / node_count
    factor = jnp.linalg.cholesky(gram_matrix)
    ortho_basis = lax.linalg.triangular_solve(
        factor, current, left_side=False, lower=True, transpose_a=True
    )
    half_solved = lax.linalg.triangular_solve(factor, rayleigh, left_side=True, lower=True)
    projected = lax.linalg.triangular_solve(
        factor, half_solved, left_side=False, lower=True, transpose_a=True
    )
    return (ortho_basis, projected)


def solution(mesh):
    in_specs = (
        P("row", "col", None, None),
        P("row", "col"),
        P(("row", "col")),
        P(("row", "col"), None),
        P(("row", "col"), None),
        P(),
        P(),
    )
    out_specs = (P(("row", "col"), None), P())
    return jax.shard_map(local, mesh=mesh, in_specs=in_specs, out_specs=out_specs, check_vma=False)
```

```python
import jax
import jax.numpy as jnp
from jax import lax
from jax.sharding import PartitionSpec as P

DEGREE = 4


def split_bf16(value):
    upper = value.astype(jnp.bfloat16)
    lower = (value - upper.astype(jnp.float32)).astype(jnp.bfloat16)
    return upper, lower


def split_dot(left, right_f32):
    upper, lower = split_bf16(right_f32)
    first = jnp.dot(left, upper, preferred_element_type=jnp.float32)
    return first + jnp.dot(left, lower, preferred_element_type=jnp.float32)


def butterfly_sum(value, axis):
    size = lax.axis_size(axis)
    if size & (size - 1):
        return lax.psum(value, axis)
    step = 1
    while step < size:
        pairs = [(index, index ^ step) for index in range(size)]
        value = value + lax.ppermute(value, axis, pairs)
        step *= 2
    return value


def all_sum(value):
    return butterfly_sum(butterfly_sum(value, "col"), "row")


def scatter_sum(value, axis):
    size = lax.axis_size(axis)
    here = lax.axis_index(axis)
    blocks = value.reshape(size, value.shape[0] // size, value.shape[1])
    total = jnp.take(blocks, here, axis=0)
    for shift in range(1, size):
        part = jnp.take(blocks, (here + shift) % size, axis=0)
        pairs = [(index, (index + shift) % size) for index in range(size)]
        total = total + lax.ppermute(part, axis, pairs)
    return total


def halving_scatter_sum(value, axis):
    size = lax.axis_size(axis)
    if size & (size - 1):
        return scatter_sum(value, axis)
    here = lax.axis_index(axis)
    rows = value.shape[0] // size
    blocks = value.reshape(size, rows, value.shape[1])
    step = 1
    while step < size:
        bit = (here // step) % 2
        paired = blocks.reshape(blocks.shape[0] // 2, 2, rows, value.shape[1])
        kept = lax.dynamic_index_in_dim(paired, bit, axis=1, keepdims=False)
        sent = lax.dynamic_index_in_dim(paired, 1 - bit, axis=1, keepdims=False)
        pairs = [(index, index ^ step) for index in range(size)]
        blocks = kept + lax.ppermute(sent, axis, pairs)
        step *= 2
    return blocks.reshape(rows, value.shape[1])


def doubling_gather(value, axis):
    size = lax.axis_size(axis)
    if size & (size - 1):
        return lax.all_gather(value, axis, axis=0, tiled=True)
    here = lax.axis_index(axis)
    result = value
    step = 1
    while step < size:
        pairs = [(index, index ^ step) for index in range(size)]
        other = lax.ppermute(result, axis, pairs)
        low = (here // step) % 2 == 0
        result = jnp.concatenate(
            [jnp.where(low, result, other), jnp.where(low, other, result)], axis=0
        )
        step *= 2
    return result


def far_first_gather(value, axis):
    size = lax.axis_size(axis)
    if size & (size - 1):
        return lax.all_gather(value, axis, axis=0, tiled=True)
    here = lax.axis_index(axis)
    result = value[None]
    step = size // 2
    while step >= 1:
        pairs = [(index, index ^ step) for index in range(size)]
        other = lax.ppermute(result, axis, pairs)
        low = (here // step) % 2 == 0
        result = jnp.concatenate(
            [jnp.where(low, result, other), jnp.where(low, other, result)], axis=0
        )
        step //= 2
    bits = size.bit_length() - 1
    result = result.reshape((2,) * bits + value.shape)
    result = jnp.transpose(result, tuple(reversed(range(bits))) + (bits, bits + 1))
    return result.reshape(-1, value.shape[1])


def local(tiles, tile_cols, degree_scale, start_block, planted, strengths, bounds):
    piece_rows = start_block.shape[0]
    node_count = piece_rows * lax.axis_size("row") * lax.axis_size("col")
    tile_rows, slots, tile_size = tiles.shape[0], tiles.shape[1], tiles.shape[2]
    n_blocks = lax.axis_size("row") * piece_rows // tile_size
    weights = strengths[:, None]

    onehot = (tile_cols[:, :, None] == jnp.arange(n_blocks, dtype=jnp.int32)[None, None, :]).astype(jnp.bfloat16)
    dense = jnp.einsum("rst,rsab->ratb", onehot, tiles, preferred_element_type=jnp.float32)
    dense = dense.reshape(tile_rows * tile_size, n_blocks * tile_size)
    w_hi, w_lo = split_bf16(dense)
    w_both = jnp.concatenate([w_hi, w_lo], axis=1)

    planted_cols = doubling_gather(planted, "row")
    planted_rows = far_first_gather(planted, "col")

    def operate(vector):
        scaled = (degree_scale[:, None] * vector).astype(jnp.bfloat16)
        gathered = doubling_gather(scaled, "row")
        product = jnp.dot(
            w_both, jnp.concatenate([gathered, gathered], axis=0), preferred_element_type=jnp.float32
        )
        partial = lax.dot_general(
            planted_cols, gathered, (((0,), (0,)), ((), ())), preferred_element_type=jnp.float32
        )
        product = product + split_dot(planted_rows, weights * partial) / node_count
        summed = halving_scatter_sum(product, "col")
        return degree_scale[:, None] * summed

    center = (bounds[1] + bounds[0]) * 0.5
    half_width = (bounds[1] - bounds[0]) * 0.5
    previous = start_block
    current = (operate(start_block) - center * start_block) / half_width
    for index_step in range(DEGREE - 1):
        applied = operate(current)
        following = 2.0 * (applied - center * current) / half_width - previous
        previous, current = (current, following)
    local_gram = jnp.dot(current.T, current, precision=lax.Precision.HIGHEST)
    applied = operate(current)
    local_rayleigh = jnp.dot(current.T, applied, precision=lax.Precision.HIGHEST)
    totals = all_sum(jnp.concatenate([local_gram, local_rayleigh], axis=0))
    gram_total, rayleigh_total = totals[: local_gram.shape[0]], totals[local_gram.shape[0] :]
    gram_matrix = gram_total / node_count
    rayleigh = rayleigh_total / node_count
    factor = jnp.linalg.cholesky(gram_matrix)
    ortho_basis = lax.linalg.triangular_solve(
        factor, current, left_side=False, lower=True, transpose_a=True
    )
    half_solved = lax.linalg.triangular_solve(factor, rayleigh, left_side=True, lower=True)
    projected = lax.linalg.triangular_solve(
        factor, half_solved, left_side=False, lower=True, transpose_a=True
    )
    return (ortho_basis, projected)


def solution(mesh):
    in_specs = (
        P("row", "col", None, None),
        P("row", "col"),
        P(("row", "col")),
        P(("row", "col"), None),
        P(("row", "col"), None),
        P(),
        P(),
    )
    out_specs = (P(("row", "col"), None), P())
    return jax.shard_map(local, mesh=mesh, in_specs=in_specs, out_specs=out_specs, check_vma=False)
```

```python
import jax
import jax.numpy as jnp
from jax import lax
from jax.sharding import PartitionSpec as P

DEGREE = 4


def split_bf16(value):
    upper = value.astype(jnp.bfloat16)
    lower = (value - upper.astype(jnp.float32)).astype(jnp.bfloat16)
    return upper, lower


def split_dot(left, right_f32):
    upper, lower = split_bf16(right_f32)
    first = jnp.dot(left, upper, preferred_element_type=jnp.float32)
    return first + jnp.dot(left, lower, preferred_element_type=jnp.float32)


def butterfly_sum(value, axis):
    size = lax.axis_size(axis)
    if size & (size - 1):
        return lax.psum(value, axis)
    step = 1
    while step < size:
        pairs = [(index, index ^ step) for index in range(size)]
        value = value + lax.ppermute(value, axis, pairs)
        step *= 2
    return value


def all_sum(value):
    return butterfly_sum(butterfly_sum(value, "col"), "row")


def scatter_sum(value, axis):
    size = lax.axis_size(axis)
    here = lax.axis_index(axis)
    blocks = value.reshape(size, value.shape[0] // size, value.shape[1])
    total = jnp.take(blocks, here, axis=0)
    for shift in range(1, size):
        part = jnp.take(blocks, (here + shift) % size, axis=0)
        pairs = [(index, (index + shift) % size) for index in range(size)]
        total = total + lax.ppermute(part, axis, pairs)
    return total


def halving_scatter_sum(value, axis):
    size = lax.axis_size(axis)
    if size & (size - 1):
        return scatter_sum(value, axis)
    here = lax.axis_index(axis)
    rows = value.shape[0] // size
    blocks = value.reshape(size, rows, value.shape[1])
    step = 1
    while step < size:
        bit = (here // step) % 2
        paired = blocks.reshape(blocks.shape[0] // 2, 2, rows, value.shape[1])
        kept = lax.dynamic_index_in_dim(paired, bit, axis=1, keepdims=False)
        sent = lax.dynamic_index_in_dim(paired, 1 - bit, axis=1, keepdims=False)
        pairs = [(index, index ^ step) for index in range(size)]
        blocks = kept + lax.ppermute(sent, axis, pairs)
        step *= 2
    return blocks.reshape(rows, value.shape[1])


def doubling_gather(value, axis):
    size = lax.axis_size(axis)
    if size & (size - 1):
        return lax.all_gather(value, axis, axis=0, tiled=True)
    here = lax.axis_index(axis)
    result = value
    step = 1
    while step < size:
        pairs = [(index, index ^ step) for index in range(size)]
        other = lax.ppermute(result, axis, pairs)
        low = (here // step) % 2 == 0
        result = jnp.concatenate(
            [jnp.where(low, result, other), jnp.where(low, other, result)], axis=0
        )
        step *= 2
    return result


def far_first_gather(value, axis):
    size = lax.axis_size(axis)
    if size & (size - 1):
        return lax.all_gather(value, axis, axis=0, tiled=True)
    here = lax.axis_index(axis)
    result = value[None]
    step = size // 2
    while step >= 1:
        pairs = [(index, index ^ step) for index in range(size)]
        other = lax.ppermute(result, axis, pairs)
        low = (here // step) % 2 == 0
        result = jnp.concatenate(
            [jnp.where(low, result, other), jnp.where(low, other, result)], axis=0
        )
        step //= 2
    bits = size.bit_length() - 1
    result = result.reshape((2,) * bits + value.shape)
    result = jnp.transpose(result, tuple(reversed(range(bits))) + (bits, bits + 1))
    return result.reshape(-1, value.shape[1])


def local(tiles, tile_cols, degree_scale, start_block, planted, strengths, bounds):
    piece_rows = start_block.shape[0]
    node_count = piece_rows * lax.axis_size("row") * lax.axis_size("col")
    tile_rows, slots, tile_size = tiles.shape[0], tiles.shape[1], tiles.shape[2]
    n_blocks = lax.axis_size("row") * piece_rows // tile_size
    weights = strengths[:, None]

    onehot = (tile_cols[:, :, None] == jnp.arange(n_blocks, dtype=jnp.int32)[None, None, :]).astype(jnp.bfloat16)
    dense = jnp.einsum("rst,rsab->ratb", onehot, tiles, preferred_element_type=jnp.float32)
    dense = dense.reshape(tile_rows * tile_size, n_blocks * tile_size)
    w_hi, w_lo = split_bf16(dense)

    planted_cols = doubling_gather(planted, "row")
    planted_rows = far_first_gather(planted, "col")

    def operate(vector):
        scaled = (degree_scale[:, None] * vector).astype(jnp.bfloat16)
        gathered = doubling_gather(scaled, "row")
        product = jnp.dot(w_hi, gathered, preferred_element_type=jnp.float32)
        product = product + jnp.dot(w_lo, gathered, preferred_element_type=jnp.float32)
        partial = lax.dot_general(
            planted_cols, gathered, (((0,), (0,)), ((), ())), preferred_element_type=jnp.float32
        )
        product = product + split_dot(planted_rows, weights * partial / node_count)
        summed = halving_scatter_sum(product, "col")
        return degree_scale[:, None] * summed

    center = (bounds[1] + bounds[0]) * 0.5
    half_width = (bounds[1] - bounds[0]) * 0.5
    previous = start_block
    current = (operate(start_block) - center * start_block) / half_width
    for index_step in range(DEGREE - 1):
        applied = operate(current)
        following = 2.0 * (applied - center * current) / half_width - previous
        previous, current = (current, following)
    local_gram = jnp.dot(current.T, current, precision=lax.Precision.HIGHEST)
    applied = operate(current)
    local_rayleigh = jnp.dot(current.T, applied, precision=lax.Precision.HIGHEST)
    totals = all_sum(jnp.concatenate([local_gram, local_rayleigh], axis=0))
    gram_total, rayleigh_total = totals[: local_gram.shape[0]], totals[local_gram.shape[0] :]
    gram_matrix = gram_total / node_count
    rayleigh = rayleigh_total / node_count
    factor = jnp.linalg.cholesky(gram_matrix)
    ortho_basis = lax.linalg.triangular_solve(
        factor, current, left_side=False, lower=True, transpose_a=True
    )
    half_solved = lax.linalg.triangular_solve(factor, rayleigh, left_side=True, lower=True)
    projected = lax.linalg.triangular_solve(
        factor, half_solved, left_side=False, lower=True, transpose_a=True
    )
    return (ortho_basis, projected)


def solution(mesh):
    in_specs = (
        P("row", "col", None, None),
        P("row", "col"),
        P(("row", "col")),
        P(("row", "col"), None),
        P(("row", "col"), None),
        P(),
        P(),
    )
    out_specs = (P(("row", "col"), None), P())
    return jax.shard_map(local, mesh=mesh, in_specs=in_specs, out_specs=out_specs, check_vma=False)
```

```python
import jax
import jax.numpy as jnp
from jax import lax
from jax.sharding import PartitionSpec as P

DEGREE = 4


def split_bf16(value):
    upper = value.astype(jnp.bfloat16)
    lower = (value - upper.astype(jnp.float32)).astype(jnp.bfloat16)
    return upper, lower


def split_dot(left, right_f32):
    upper, lower = split_bf16(right_f32)
    first = jnp.dot(left, upper, preferred_element_type=jnp.float32)
    return first + jnp.dot(left, lower, preferred_element_type=jnp.float32)


def butterfly_sum(value, axis):
    size = lax.axis_size(axis)
    if size & (size - 1):
        return lax.psum(value, axis)
    step = 1
    while step < size:
        pairs = [(index, index ^ step) for index in range(size)]
        value = value + lax.ppermute(value, axis, pairs)
        step *= 2
    return value


def all_sum(value):
    return butterfly_sum(butterfly_sum(value, "col"), "row")


def scatter_sum(value, axis):
    size = lax.axis_size(axis)
    here = lax.axis_index(axis)
    blocks = value.reshape(size, value.shape[0] // size, value.shape[1])
    total = jnp.take(blocks, here, axis=0)
    for shift in range(1, size):
        part = jnp.take(blocks, (here + shift) % size, axis=0)
        pairs = [(index, (index + shift) % size) for index in range(size)]
        total = total + lax.ppermute(part, axis, pairs)
    return total


def halving_scatter_sum(value, axis):
    size = lax.axis_size(axis)
    if size & (size - 1):
        return scatter_sum(value, axis)
    here = lax.axis_index(axis)
    rows = value.shape[0] // size
    blocks = value.reshape(size, rows, value.shape[1])
    step = 1
    while step < size:
        bit = (here // step) % 2
        paired = blocks.reshape(blocks.shape[0] // 2, 2, rows, value.shape[1])
        kept = lax.dynamic_index_in_dim(paired, bit, axis=1, keepdims=False)
        sent = lax.dynamic_index_in_dim(paired, 1 - bit, axis=1, keepdims=False)
        pairs = [(index, index ^ step) for index in range(size)]
        blocks = kept + lax.ppermute(sent, axis, pairs)
        step *= 2
    return blocks.reshape(rows, value.shape[1])


def doubling_gather(value, axis):
    size = lax.axis_size(axis)
    if size & (size - 1):
        return lax.all_gather(value, axis, axis=0, tiled=True)
    here = lax.axis_index(axis)
    result = value
    step = 1
    while step < size:
        pairs = [(index, index ^ step) for index in range(size)]
        other = lax.ppermute(result, axis, pairs)
        low = (here // step) % 2 == 0
        result = jnp.concatenate(
            [jnp.where(low, result, other), jnp.where(low, other, result)], axis=0
        )
        step *= 2
    return result


def far_first_gather(value, axis):
    size = lax.axis_size(axis)
    if size & (size - 1):
        return lax.all_gather(value, axis, axis=0, tiled=True)
    here = lax.axis_index(axis)
    result = value[None]
    step = size // 2
    while step >= 1:
        pairs = [(index, index ^ step) for index in range(size)]
        other = lax.ppermute(result, axis, pairs)
        low = (here // step) % 2 == 0
        result = jnp.concatenate(
            [jnp.where(low, result, other), jnp.where(low, other, result)], axis=0
        )
        step //= 2
    bits = size.bit_length() - 1
    result = result.reshape((2,) * bits + value.shape)
    result = jnp.transpose(result, tuple(reversed(range(bits))) + (bits, bits + 1))
    return result.reshape(-1, value.shape[1])


def local(tiles, tile_cols, degree_scale, start_block, planted, strengths, bounds):
    piece_rows = start_block.shape[0]
    node_count = piece_rows * lax.axis_size("row") * lax.axis_size("col")
    tile_rows, slots, tile_size = tiles.shape[0], tiles.shape[1], tiles.shape[2]
    n_blocks = lax.axis_size("row") * piece_rows // tile_size
    weights = strengths[:, None]

    onehot = (tile_cols[:, :, None] == jnp.arange(n_blocks, dtype=jnp.int32)[None, None, :]).astype(jnp.bfloat16)
    dense = jnp.einsum("rst,rsab->ratb", onehot, tiles, preferred_element_type=jnp.float32)
    dense = dense.reshape(tile_rows * tile_size, n_blocks * tile_size)
    w_hi, w_lo = split_bf16(dense)

    planted_cols = doubling_gather(planted, "row")
    planted_rows = far_first_gather(planted, "col")

    def operate(vector):
        scaled = (degree_scale[:, None] * vector).astype(jnp.bfloat16)
        gathered = doubling_gather(scaled, "row")
        product = jnp.dot(w_hi, gathered, preferred_element_type=jnp.float32)
        product = product + jnp.dot(w_lo, gathered, preferred_element_type=jnp.float32)
        partial = lax.dot_general(
            planted_cols, gathered, (((0,), (0,)), ((), ())), preferred_element_type=jnp.float32
        )
        product = product + split_dot(planted_rows, weights * partial / node_count)
        summed = halving_scatter_sum(product, "col")
        return degree_scale[:, None] * summed

    center = (bounds[1] + bounds[0]) * 0.5
    half_width = (bounds[1] - bounds[0]) * 0.5
    previous = start_block
    current = (operate(start_block) - center * start_block) / half_width
    for index_step in range(DEGREE - 1):
        applied = operate(current)
        following = 2.0 * (applied - center * current) / half_width - previous
        previous, current = (current, following)
    applied = operate(current)
    both = jnp.dot(current.T, jnp.concatenate([current, applied], axis=1), precision=lax.Precision.HIGHEST)
    totals = all_sum(both)
    gram_total, rayleigh_total = totals[:, : current.shape[1]], totals[:, current.shape[1] :]
    gram_matrix = gram_total / node_count
    rayleigh = rayleigh_total / node_count
    factor = jnp.linalg.cholesky(gram_matrix)
    ortho_basis = lax.linalg.triangular_solve(
        factor, current, left_side=False, lower=True, transpose_a=True
    )
    half_solved = lax.linalg.triangular_solve(factor, rayleigh, left_side=True, lower=True)
    projected = lax.linalg.triangular_solve(
        factor, half_solved, left_side=False, lower=True, transpose_a=True
    )
    return (ortho_basis, projected)


def solution(mesh):
    in_specs = (
        P("row", "col", None, None),
        P("row", "col"),
        P(("row", "col")),
        P(("row", "col"), None),
        P(("row", "col"), None),
        P(),
        P(),
    )
    out_specs = (P(("row", "col"), None), P())
    return jax.shard_map(local, mesh=mesh, in_specs=in_specs, out_specs=out_specs, check_vma=False)
```
